32 devices in a mesh: mem: 4 (over y, x), tile: 8 (over z, core).
Axes of the slice: x: 2, y: 2, z: 4, core: 2. Of those that a mesh axis runs over, the one named last changes fastest.
Arguments:
- controls: float32 [32, 128, 1792], P('mem', 'tile'), may hold values from -6 to 6
- perturbations: bfloat16 [32, 4, 128, 1792], P('mem', None, 'tile'), may hold values from -1.5 to 1.5
- jacobian: float32 [4, 128, 1792], P(None, 'tile'), may hold values from -3 to 3
- obs_weight: float32 [128, 1792], P('tile'), may hold values from 0.5 to 4
- radar_mask: int32 [128, 1792], P('tile'), may hold values 0 or 1
- row_faces: float32 [128, 1792], P('tile'), may hold values from 0.12 to 0.25
- col_faces: float32 [128, 1792], P('tile'), may hold values from 0.12 to 0.25
Outputs:
- gradient: float32 [32, 128, 1792], P('mem', 'tile')
The draws below stay inside these ranges and needn't reach their ends.
All inputs are finite; a program needn't handle non-finite values. No bound on the sum of `radar_mask` on one device may be relied on, other than what follows from the above.
Results may differ from the reference program's by a relative error of at most 0.0003.
Values sent between devices are 32-bit elements; how exact they have to be, the bound alone decides.
No kernel may reach another device: no remote copies, remote signals or barrier semaphores. Data moves between devices by JAX's collectives and lax.ppermute only.
A program may use at most 64 MiB of HBM per device.

```python
import math
import jax
import jax.numpy as jnp
from jax import lax

MEMBERS = 32
VARS = 4
COLS = 1792
STEPS = 4
ROWS = 128


def with_ends(drawn, rng, low, largest):
    longest = drawn.shape.index(max(drawn.shape))
    spots = []
    for shift in (0, 1):
        where = [jax.random.randint(jax.random.fold_in(rng, axis), (), 0, length) for axis, length in enumerate(drawn.shape)]
        where[longest] = (where[longest] + shift) % drawn.shape[longest]
        spots.append(tuple(where))
    return drawn.at[spots[0]].set(low).at[spots[1]].set(largest)


def block_scale(stream_key, extent, shards, low, largest):
    loudness, own = 1.0, jax.random.fold_in(stream_key, 6)
    for position, shards_of in shards:
        heights = jnp.exp(jax.random.uniform(jax.random.fold_in(own, position), (shards_of,), jnp.float32, low / len(shards), largest / len(shards)))
        loudness = loudness * jnp.repeat(heights, extent[position] // shards_of).reshape([-1 if axis == position else 1 for axis in range(len(extent))])
    return loudness


def bell_draw(stream_key, extent, scale, bound, shards=(), dtype=jnp.bfloat16):
    result = scale * jax.random.normal(stream_key, extent, jnp.float32)
    if shards:
        result = result * block_scale(stream_key, extent, shards, -0.22, 0.18)
    return jnp.clip(result, -bound, bound).astype(dtype)


def setup_inputs(seed: int = 0) -> dict:
    key_of = jax.random.split(jax.random.key(seed), 8)
    return {
        "controls": bell_draw(key_of[0], (MEMBERS, ROWS, COLS), 1.0, 6.0, ((0, 4), (1, 8)), jnp.float32),
        "perturbations": bell_draw(key_of[1], (MEMBERS, VARS, ROWS, COLS), 0.25, 1.5, ((0, 4), (2, 8))),
        "jacobian": bell_draw(key_of[2], (VARS, ROWS, COLS), 0.5, 3.0, ((1, 8),), jnp.float32),
        "obs_weight": jnp.clip(jnp.exp(math.log(4.0) - 2.0794415 * jax.random.uniform(key_of[3], (ROWS, COLS), jnp.float32) ** block_scale(key_of[3], (ROWS, COLS), ((0, 8),), -0.2, 0.2)), 0.5, 4.0),
        "radar_mask": with_ends((jax.random.randint(key_of[4], (ROWS, COLS), 0, 2) < 1).astype(jnp.int32), jax.random.fold_in(key_of[4], 1), 0, 1),
        "row_faces": jnp.clip(0.12 + 0.13 * jax.random.uniform(key_of[5], (ROWS, COLS), jnp.float32) ** block_scale(key_of[5], (ROWS, COLS), ((0, 8),), -0.2, 0.2), 0.12, 0.25),
        "col_faces": jnp.clip(0.12 + 0.13 * jax.random.uniform(key_of[6], (ROWS, COLS), jnp.float32) ** block_scale(key_of[6], (ROWS, COLS), ((0, 8),), -0.2, 0.2), 0.12, 0.25),
    }


def diffuse(values, row_coef, col_coef):
    row_flux = row_coef[..., :-1, :] * (values[..., 1:, :] - values[..., :-1, :])
    col_flux = col_coef[..., :, :-1] * (values[..., :, 1:] - values[..., :, :-1])
    zeros_row = jnp.zeros_like(values[..., :1, :])
    zeros_col = jnp.zeros_like(values[..., :, :1])
    values = values + jnp.concatenate([row_flux, zeros_row], -2) - jnp.concatenate([zeros_row, row_flux], -2)
    return values + jnp.concatenate([col_flux, zeros_col], -1) - jnp.concatenate([zeros_col, col_flux], -1)


def reference(controls, perturbations, jacobian, obs_weight, radar_mask, row_faces, col_faces):
    row_index = lax.broadcasted_iota(jnp.int32, row_faces.shape, 0)
    row_coef = jnp.where(row_index < row_faces.shape[0] - 1, row_faces, jnp.zeros_like(row_faces))
    col_coef = col_faces

    def localize(field):
        for repeat in range(STEPS):
            field = diffuse(field, row_coef, col_coef)
        return field

    def accumulate(carry, member):
        control, spread = member
        localized = localize(control)
        return carry + spread.astype(jnp.float32) * localized[None], None

    increment, _ = lax.scan(accumulate, jnp.zeros(jacobian.shape, jnp.float32), (controls, perturbations))
    reflect = jnp.sum(jacobian * increment, 0)
    weighted = radar_mask.astype(jnp.float32) * obs_weight * reflect
    adjoint_inc = jacobian * weighted[None]

    def backward(member):
        control, spread = member
        sensitivity = jnp.sum(spread.astype(jnp.float32) * adjoint_inc, 0)
        return control + localize(sensitivity)

    return lax.map(backward, (controls, perturbations))
```

```python
import jax
import jax.numpy as jnp
from jax import lax
from jax.sharding import PartitionSpec as P

STEPS = 4


def padded(cells, sides, width):
    for axis, dim in sides:
        count = lax.axis_size(axis)
        ends = count - 1
        head = lax.slice_in_dim(cells, 0, width, axis=dim)
        tail = lax.slice_in_dim(cells, cells.shape[dim] - width, cells.shape[dim], axis=dim)
        cells = jnp.concatenate(
            [
                lax.ppermute(tail, axis, [(i, (i + 1) % count) for i in range(ends)]),
                cells,
                lax.ppermute(head, axis, [((i + 1) % count, i) for i in range(ends)]),
            ],
            axis=dim,
        )
    return cells


def diffuse(values, row_coef, col_coef):
    row_flux = row_coef[..., :-1, :] * (values[..., 1:, :] - values[..., :-1, :])
    col_flux = col_coef[..., :, :-1] * (values[..., :, 1:] - values[..., :, :-1])
    zeros_row = jnp.zeros_like(values[..., :1, :])
    zeros_col = jnp.zeros_like(values[..., :, :1])
    values = (
        values
        + jnp.concatenate([row_flux, zeros_row], -2)
        - jnp.concatenate([zeros_row, row_flux], -2)
    )
    return (
        values
        + jnp.concatenate([col_flux, zeros_col], -1)
        - jnp.concatenate([zeros_col, col_flux], -1)
    )


def localize(field, coef_band):
    row_count = field.shape[1]
    widened = padded(field, (("tile", 1),), STEPS)
    for repeat in range(STEPS):
        widened = diffuse(widened, coef_band[0], coef_band[1])
    field = widened[:, STEPS : STEPS + row_count]
    return field


def per_device(controls, perturbations, jacobian, obs_weight, radar_mask, row_faces, col_faces):
    row_count = controls.shape[1]
    row_index = lax.axis_index("tile") * row_count + lax.broadcasted_iota(
        jnp.int32, row_faces.shape, 0
    )
    row_coef = jnp.where(
        row_index < row_count * lax.axis_size("tile") - 1, row_faces, jnp.zeros_like(row_faces)
    )
    stacked = jnp.stack([row_coef, col_faces])
    coef_band = padded(stacked, (("tile", 1),), STEPS)
    localized = localize(controls, coef_band)
    member_sum = jnp.sum(perturbations * localized[:, None], axis=0)
    weights = radar_mask.astype(jnp.float32) * obs_weight
    reflect = lax.psum(jnp.sum(jacobian * member_sum, 0), "mem")
    adjoint_inc = jacobian * (weights * reflect)[None]
    sensitivity = jnp.sum(perturbations * adjoint_inc[None], axis=1)
    return controls + localize(sensitivity, coef_band)


def solution(mesh):
    placed = (
        P("mem", "tile", None),
        P("mem", None, "tile", None),
        P(None, "tile", None),
        P("tile", None),
        P("tile", None),
        P("tile", None),
        P("tile", None),
    )
    return jax.shard_map(
        per_device, mesh=mesh, in_specs=placed, out_specs=P("mem", "tile", None), check_vma=False
    )
```

```python
import jax
import jax.numpy as jnp
from jax import lax
from jax.sharding import PartitionSpec as P

STEPS = 4


def padded(cells, sides, width):
    for axis, dim in sides:
        count = lax.axis_size(axis)
        ends = count - 1
        head = lax.slice_in_dim(cells, 0, width, axis=dim)
        tail = lax.slice_in_dim(cells, cells.shape[dim] - width, cells.shape[dim], axis=dim)
        cells = jnp.concatenate(
            [
                lax.ppermute(tail, axis, [(i, (i + 1) % count) for i in range(ends)]),
                cells,
                lax.ppermute(head, axis, [((i + 1) % count, i) for i in range(ends)]),
            ],
            axis=dim,
        )
    return cells


def mem_sum(part):
    count = lax.axis_size("mem")
    if count & (count - 1):
        return lax.psum(part, "mem")
    stride = 1
    while stride < count:
        part = part + lax.ppermute(part, "mem", [(i, i ^ stride) for i in range(count)])
        stride *= 2
    return part


def diffuse(values, row_coef, col_coef):
    row_flux = row_coef[..., :-1, :] * (values[..., 1:, :] - values[..., :-1, :])
    col_flux = col_coef[..., :, :-1] * (values[..., :, 1:] - values[..., :, :-1])
    zeros_row = jnp.zeros_like(values[..., :1, :])
    zeros_col = jnp.zeros_like(values[..., :, :1])
    values = (
        values
        + jnp.concatenate([row_flux, zeros_row], -2)
        - jnp.concatenate([zeros_row, row_flux], -2)
    )
    return (
        values
        + jnp.concatenate([col_flux, zeros_col], -1)
        - jnp.concatenate([zeros_col, col_flux], -1)
    )


def localize(field, coef_band):
    row_count = field.shape[1]
    widened = padded(field, (("tile", 1),), STEPS)
    for repeat in range(STEPS):
        widened = diffuse(widened, coef_band[0], coef_band[1])
    field = widened[:, STEPS : STEPS + row_count]
    return field


def per_device(controls, perturbations, jacobian, obs_weight, radar_mask, row_faces, col_faces):
    row_count = controls.shape[1]
    row_index = lax.axis_index("tile") * row_count + lax.broadcasted_iota(
        jnp.int32, row_faces.shape, 0
    )
    row_coef = jnp.where(
        row_index < row_count * lax.axis_size("tile") - 1, row_faces, jnp.zeros_like(row_faces)
    )
    stacked = jnp.stack([row_coef, col_faces])
    coef_band = padded(stacked, (("tile", 1),), STEPS)
    localized = localize(controls, coef_band)
    member_sum = jnp.sum(perturbations * localized[:, None], axis=0)
    weights = radar_mask.astype(jnp.float32) * obs_weight
    reflect = mem_sum(jnp.sum(jacobian * member_sum, 0))
    adjoint_inc = jacobian * (weights * reflect)[None]
    sensitivity = jnp.sum(perturbations * adjoint_inc[None], axis=1)
    return controls + localize(sensitivity, coef_band)


def solution(mesh):
    placed = (
        P("mem", "tile", None),
        P("mem", None, "tile", None),
        P(None, "tile", None),
        P("tile", None),
        P("tile", None),
        P("tile", None),
        P("tile", None),
    )
    return jax.shard_map(
        per_device, mesh=mesh, in_specs=placed, out_specs=P("mem", "tile", None), check_vma=False
    )
```

```python
import jax
import jax.numpy as jnp
from jax import lax
from jax.sharding import PartitionSpec as P

STEPS = 4


def exchange(parts, width):
    count = lax.axis_size("tile")
    cols = parts[0].shape[-1]
    sizes = [part[..., :width, :].size // cols for part in parts]
    head = jnp.concatenate([part[..., :width, :].reshape(-1, cols) for part in parts], 0)
    tail = jnp.concatenate([part[..., -width:, :].reshape(-1, cols) for part in parts], 0)
    above = lax.ppermute(tail, "tile", [(i, i + 1) for i in range(count - 1)])
    below = lax.ppermute(head, "tile", [(i + 1, i) for i in range(count - 1)])
    bands = []
    start = 0
    for part, size in zip(parts, sizes):
        shape = part.shape[:-2] + (width, cols)
        top = above[start : start + size].reshape(shape)
        bottom = below[start : start + size].reshape(shape)
        bands.append(jnp.concatenate([top, part, bottom], -2))
        start += size
    return bands


def mem_sum(part):
    count = lax.axis_size("mem")
    if count & (count - 1):
        return lax.psum(part, "mem")
    stride = 1
    while stride < count:
        part = part + lax.ppermute(part, "mem", [(i, i ^ stride) for i in range(count)])
        stride *= 2
    return part


def diffuse(values, row_coef, col_coef):
    row_flux = row_coef[..., :-1, :] * (values[..., 1:, :] - values[..., :-1, :])
    col_flux = col_coef[..., :, :-1] * (values[..., :, 1:] - values[..., :, :-1])
    zeros_row = jnp.zeros_like(values[..., :1, :])
    zeros_col = jnp.zeros_like(values[..., :, :1])
    values = (
        values
        + jnp.concatenate([row_flux, zeros_row], -2)
        - jnp.concatenate([zeros_row, row_flux], -2)
    )
    return (
        values
        + jnp.concatenate([col_flux, zeros_col], -1)
        - jnp.concatenate([zeros_col, col_flux], -1)
    )


def localize(field, coef_band):
    for repeat in range(STEPS):
        field = diffuse(field, coef_band[0], coef_band[1])
    return field


def per_device(controls, perturbations, jacobian, obs_weight, radar_mask, row_faces, col_faces):
    row_count = controls.shape[1]
    row_index = lax.axis_index("tile") * row_count + lax.broadcasted_iota(
        jnp.int32, row_faces.shape, 0
    )
    row_coef = jnp.where(
        row_index < row_count * lax.axis_size("tile") - 1, row_faces, jnp.zeros_like(row_faces)
    )
    stacked = jnp.stack([row_coef, col_faces])
    field, coef_band = exchange([controls, stacked], STEPS)
    localized = localize(field, coef_band)[:, STEPS : STEPS + row_count]
    mix = jnp.sum(perturbations.astype(jnp.float32) * jacobian[None], axis=1)
    (mix_band,) = exchange([mix], STEPS)
    reflect = mem_sum(jnp.sum(mix * localized, 0))
    weighted = radar_mask.astype(jnp.float32) * obs_weight * reflect
    (weighted_band,) = exchange([weighted[None]], STEPS)
    sensitivity = mix_band * weighted_band
    return controls + localize(sensitivity, coef_band)[:, STEPS : STEPS + row_count]


def solution(mesh):
    placed = (
        P("mem", "tile", None),
        P("mem", None, "tile", None),
        P(None, "tile", None),
        P("tile", None),
        P("tile", None),
        P("tile", None),
        P("tile", None),
    )
    return jax.shard_map(
        per_device, mesh=mesh, in_specs=placed, out_specs=P("mem", "tile", None), check_vma=False
    )
```

```python
import jax
import jax.numpy as jnp
from jax import lax
from jax.sharding import PartitionSpec as P

STEPS = 4


def exchange(parts, width):
    count = lax.axis_size("tile")
    cols = parts[0].shape[-1]
    sizes = [part[..., :width, :].size // cols for part in parts]
    head = jnp.concatenate([part[..., :width, :].reshape(-1, cols) for part in parts], 0)
    tail = jnp.concatenate([part[..., -width:, :].reshape(-1, cols) for part in parts], 0)
    above = lax.ppermute(tail, "tile", [(i, i + 1) for i in range(count - 1)])
    below = lax.ppermute(head, "tile", [(i + 1, i) for i in range(count - 1)])
    bands = []
    start = 0
    for part, size in zip(parts, sizes):
        shape = part.shape[:-2] + (width, cols)
        top = above[start : start + size].reshape(shape)
        bottom = below[start : start + size].reshape(shape)
        bands.append(jnp.concatenate([top, part, bottom], -2))
        start += size
    return bands


def mem_sum(part):
    count = lax.axis_size("mem")
    if count & (count - 1) or part.shape[-1] % 256:
        return lax.psum(part, "mem")
    half = part.shape[-1] // 2
    first, second = part[..., :half], part[..., half:]
    strides = []
    stride = 1
    while stride < count:
        strides.append(stride)
        stride *= 2
    for up, down in zip(strides, strides[::-1]):
        first = first + lax.ppermute(first, "mem", [(i, i ^ up) for i in range(count)])
        second = second + lax.ppermute(second, "mem", [(i, i ^ down) for i in range(count)])
    return jnp.concatenate([first, second], -1)


def diffuse(values, row_coef, col_coef):
    row_flux = row_coef[..., :-1, :] * (values[..., 1:, :] - values[..., :-1, :])
    col_flux = col_coef[..., :, :-1] * (values[..., :, 1:] - values[..., :, :-1])
    zeros_row = jnp.zeros_like(values[..., :1, :])
    zeros_col = jnp.zeros_like(values[..., :, :1])
    values = (
        values
        + jnp.concatenate([row_flux, zeros_row], -2)
        - jnp.concatenate([zeros_row, row_flux], -2)
    )
    return (
        values
        + jnp.concatenate([col_flux, zeros_col], -1)
        - jnp.concatenate([zeros_col, col_flux], -1)
    )


def localize(field, coef_band):
    for repeat in range(STEPS):
        field = diffuse(field, coef_band[0], coef_band[1])
    return field


def per_device(controls, perturbations, jacobian, obs_weight, radar_mask, row_faces, col_faces):
    row_count = controls.shape[1]
    row_index = lax.axis_index("tile") * row_count + lax.broadcasted_iota(
        jnp.int32, row_faces.shape, 0
    )
    row_coef = jnp.where(
        row_index < row_count * lax.axis_size("tile") - 1, row_faces, jnp.zeros_like(row_faces)
    )
    stacked = jnp.stack([row_coef, col_faces])
    mix = jnp.sum(perturbations.astype(jnp.float32) * jacobian[None], axis=1)
    weights = radar_mask.astype(jnp.float32) * obs_weight
    field, coef_band = exchange([controls, stacked], 2 * STEPS)
    mix_band, weights_band = exchange([mix, weights[None]], STEPS)
    reach = row_count + 2 * STEPS
    localized = localize(field, coef_band)[:, STEPS : STEPS + reach]
    reflect = mem_sum(jnp.sum(mix_band * localized, 0))
    sensitivity = mix_band * (weights_band[0] * reflect)
    spread = localize(sensitivity, coef_band[:, STEPS : STEPS + reach])
    return controls + spread[:, STEPS : STEPS + row_count]


def solution(mesh):
    placed = (
        P("mem", "tile", None),
        P("mem", None, "tile", None),
        P(None, "tile", None),
        P("tile", None),
        P("tile", None),
        P("tile", None),
        P("tile", None),
    )
    return jax.shard_map(
        per_device, mesh=mesh, in_specs=placed, out_specs=P("mem", "tile", None), check_vma=False
    )
```

```python
import jax
import jax.numpy as jnp
from jax import lax
from jax.sharding import PartitionSpec as P

STEPS = 4


def exchange(parts):
    count = lax.axis_size("tile")
    cols = parts[0][0].shape[-1]
    head = jnp.concatenate([part[..., :width, :].reshape(-1, cols) for part, width in parts], 0)
    tail = jnp.concatenate([part[..., -width:, :].reshape(-1, cols) for part, width in parts], 0)
    above = lax.ppermute(tail, "tile", [(i, i + 1) for i in range(count - 1)])
    below = lax.ppermute(head, "tile", [(i + 1, i) for i in range(count - 1)])
    bands = []
    start = 0
    for part, width in parts:
        shape = part.shape[:-2] + (width, cols)
        size = part[..., :width, :].size // cols
        top = above[start : start + size].reshape(shape)
        bottom = below[start : start + size].reshape(shape)
        bands.append(jnp.concatenate([top, part, bottom], -2))
        start += size
    return bands


def mem_sum(part):
    count = lax.axis_size("mem")
    if count & (count - 1):
        return lax.psum(part, "mem")
    stride = 1
    while stride < count:
        part = part + lax.ppermute(part, "mem", [(i, i ^ stride) for i in range(count)])
        stride *= 2
    return part


def diffuse(values, row_coef, col_coef):
    row_flux = row_coef[..., :-1, :] * (values[..., 1:, :] - values[..., :-1, :])
    col_flux = col_coef[..., :, :-1] * (values[..., :, 1:] - values[..., :, :-1])
    zeros_row = jnp.zeros_like(values[..., :1, :])
    zeros_col = jnp.zeros_like(values[..., :, :1])
    values = (
        values
        + jnp.concatenate([row_flux, zeros_row], -2)
        - jnp.concatenate([zeros_row, row_flux], -2)
    )
    return (
        values
        + jnp.concatenate([col_flux, zeros_col], -1)
        - jnp.concatenate([zeros_col, col_flux], -1)
    )


def localize(field, coef_band):
    for repeat in range(STEPS):
        field = diffuse(field, coef_band[0], coef_band[1])
    return field


def per_device(controls, perturbations, jacobian, obs_weight, radar_mask, row_faces, col_faces):
    row_count = controls.shape[1]
    row_index = lax.axis_index("tile") * row_count + lax.broadcasted_iota(
        jnp.int32, row_faces.shape, 0
    )
    row_coef = jnp.where(
        row_index < row_count * lax.axis_size("tile") - 1, row_faces, jnp.zeros_like(row_faces)
    )
    stacked = jnp.stack([row_coef, col_faces])
    mix = jnp.sum(perturbations.astype(jnp.float32) * jacobian[None], axis=1)
    weights = radar_mask.astype(jnp.float32) * obs_weight
    field, coef_band, mix_band, weights_band = exchange(
        [(controls, 2 * STEPS), (stacked, 2 * STEPS), (mix, STEPS), (weights[None], STEPS)]
    )
    reach = row_count + 2 * STEPS
    localized = localize(field, coef_band)[:, STEPS : STEPS + reach]
    reflect = mem_sum(jnp.sum(mix_band * localized, 0))
    sensitivity = mix_band * (weights_band[0] * reflect)
    spread = localize(sensitivity, coef_band[:, STEPS : STEPS + reach])
    return controls + spread[:, STEPS : STEPS + row_count]


def solution(mesh):
    placed = (
        P("mem", "tile", None),
        P("mem", None, "tile", None),
        P(None, "tile", None),
        P("tile", None),
        P("tile", None),
        P("tile", None),
        P("tile", None),
    )
    return jax.shard_map(
        per_device, mesh=mesh, in_specs=placed, out_specs=P("mem", "tile", None), check_vma=False
    )
```

```python
import jax
import jax.numpy as jnp
from jax import lax
from jax.experimental import pallas as pl
from jax.experimental.pallas import tpu as pltpu
from jax.sharding import PartitionSpec as P
import functools

STEPS = 4


def exchange(parts, width):
    count = lax.axis_size("tile")
    cols = parts[0].shape[-1]
    sizes = [part[..., :width, :].size // cols for part in parts]
    head = jnp.concatenate([part[..., :width, :].reshape(-1, cols) for part in parts], 0)
    tail = jnp.concatenate([part[..., -width:, :].reshape(-1, cols) for part in parts], 0)
    above = lax.ppermute(tail, "tile", [(i, i + 1) for i in range(count - 1)])
    below = lax.ppermute(head, "tile", [(i + 1, i) for i in range(count - 1)])
    bands = []
    start = 0
    for part, size in zip(parts, sizes):
        shape = part.shape[:-2] + (width, cols)
        top = above[start : start + size].reshape(shape)
        bottom = below[start : start + size].reshape(shape)
        bands.append(jnp.concatenate([top, part, bottom], -2))
        start += size
    return bands


def mem_sum(part):
    count = lax.axis_size("mem")
    if count & (count - 1):
        return lax.psum(part, "mem")
    stride = 1
    while stride < count:
        part = part + lax.ppermute(part, "mem", [(i, i ^ stride) for i in range(count)])
        stride *= 2
    return part


def diffuse_block(values, row_coef, col_coef):
    rows, cols = values.shape
    row_flux = row_coef * (pltpu.roll(values, rows - 1, 0) - values)
    col_flux = col_coef * (pltpu.roll(values, cols - 1, 1) - values)
    values = values + row_flux - pltpu.roll(row_flux, 1, 0)
    return values + col_flux - pltpu.roll(col_flux, 1, 1)


def forward_kernel(band_ref, coef_ref, mix_ref, out_ref):
    member = pl.program_id(0)
    values = band_ref[0]
    for repeat in range(STEPS):
        values = diffuse_block(values, coef_ref[0], coef_ref[1])
    keep = out_ref.shape[0]
    term = mix_ref[0] * pltpu.roll(values, values.shape[0] - STEPS, 0)[:keep]

    @pl.when(member == 0)
    def _():
        out_ref[...] = term

    @pl.when(member > 0)
    def _():
        out_ref[...] = out_ref[...] + term


def backward_kernel(mix_ref, weighted_ref, coef_ref, controls_ref, out_ref):
    rows = mix_ref.shape[1]
    shift = coef_ref.shape[1] - STEPS
    row_coef = pltpu.roll(coef_ref[0], shift, 0)[:rows]
    col_coef = pltpu.roll(coef_ref[1], shift, 0)[:rows]
    values = mix_ref[0] * weighted_ref[...]
    for repeat in range(STEPS):
        values = diffuse_block(values, row_coef, col_coef)
    keep = out_ref.shape[1]
    out_ref[0] = controls_ref[0] + pltpu.roll(values, rows - STEPS, 0)[:keep]


def forward(band, coef, mix):
    members, rows, cols = band.shape
    keep = mix.shape[1]
    return pl.pallas_call(
        forward_kernel,
        grid=(members,),
        in_specs=[
            pl.BlockSpec((1, rows, cols), lambda k: (k, 0, 0)),
            pl.BlockSpec((2, rows, cols), lambda k: (0, 0, 0)),
            pl.BlockSpec((1, keep, cols), lambda k: (k, 0, 0)),
        ],
        out_specs=pl.BlockSpec((keep, cols), lambda k: (0, 0)),
        out_shape=jax.ShapeDtypeStruct((keep, cols), jnp.float32),
    )(band, coef, mix)


def backward(mix, weighted, coef, controls):
    members, rows, cols = mix.shape
    keep = controls.shape[1]
    return pl.pallas_call(
        backward_kernel,
        grid=(members,),
        in_specs=[
            pl.BlockSpec((1, rows, cols), lambda k: (k, 0, 0)),
            pl.BlockSpec((rows, cols), lambda k: (0, 0)),
            pl.BlockSpec((2, coef.shape[1], cols), lambda k: (0, 0, 0)),
            pl.BlockSpec((1, keep, cols), lambda k: (k, 0, 0)),
        ],
        out_specs=pl.BlockSpec((1, keep, cols), lambda k: (k, 0, 0)),
        out_shape=jax.ShapeDtypeStruct(controls.shape, jnp.float32),
    )(mix, weighted, coef, controls)


def diffuse(values, row_coef, col_coef):
    row_flux = row_coef[..., :-1, :] * (values[..., 1:, :] - values[..., :-1, :])
    col_flux = col_coef[..., :, :-1] * (values[..., :, 1:] - values[..., :, :-1])
    zeros_row = jnp.zeros_like(values[..., :1, :])
    zeros_col = jnp.zeros_like(values[..., :, :1])
    values = (
        values
        + jnp.concatenate([row_flux, zeros_row], -2)
        - jnp.concatenate([zeros_row, row_flux], -2)
    )
    return (
        values
        + jnp.concatenate([col_flux, zeros_col], -1)
        - jnp.concatenate([zeros_col, col_flux], -1)
    )


def localize(field, coef_band):
    for repeat in range(STEPS):
        field = diffuse(field, coef_band[0], coef_band[1])
    return field


def per_device(controls, perturbations, jacobian, obs_weight, radar_mask, row_faces, col_faces):
    row_count, col_count = controls.shape[1:]
    row_index = lax.axis_index("tile") * row_count + lax.broadcasted_iota(
        jnp.int32, row_faces.shape, 0
    )
    row_coef = jnp.where(
        row_index < row_count * lax.axis_size("tile") - 1, row_faces, jnp.zeros_like(row_faces)
    )
    col_index = lax.broadcasted_iota(jnp.int32, col_faces.shape, 1)
    col_coef = jnp.where(col_index < col_count - 1, col_faces, jnp.zeros_like(col_faces))
    stacked = jnp.stack([row_coef, col_coef])
    mix = jnp.sum(perturbations.astype(jnp.float32) * jacobian[None], axis=1)
    weights = radar_mask.astype(jnp.float32) * obs_weight
    field, coef_band = exchange([controls, stacked], 2 * STEPS)
    mix_band, weights_band = exchange([mix, weights[None]], STEPS)
    reflect = mem_sum(forward(field, coef_band, mix_band))
    return backward(mix_band, weights_band[0] * reflect, coef_band, controls)


def solution(mesh):
    placed = (
        P("mem", "tile", None),
        P("mem", None, "tile", None),
        P(None, "tile", None),
        P("tile", None),
        P("tile", None),
        P("tile", None),
        P("tile", None),
    )
    return jax.shard_map(
        per_device, mesh=mesh, in_specs=placed, out_specs=P("mem", "tile", None), check_vma=False
    )
```

```python
import jax
import jax.numpy as jnp
from jax import lax
from jax.sharding import PartitionSpec as P

STEPS = 4


def exchange(parts, width):
    count = lax.axis_size("tile")
    cols = parts[0].shape[-1]
    sizes = [part[..., :width, :].size // cols for part in parts]
    head = jnp.concatenate([part[..., :width, :].reshape(-1, cols) for part in parts], 0)
    tail = jnp.concatenate([part[..., -width:, :].reshape(-1, cols) for part in parts], 0)
    above = lax.ppermute(tail, "tile", [(i, i + 1) for i in range(count - 1)])
    below = lax.ppermute(head, "tile", [(i + 1, i) for i in range(count - 1)])
    bands = []
    start = 0
    for part, size in zip(parts, sizes):
        shape = part.shape[:-2] + (width, cols)
        top = above[start : start + size].reshape(shape)
        bottom = below[start : start + size].reshape(shape)
        bands.append(jnp.concatenate([top, part, bottom], -2))
        start += size
    return bands


def mem_sum(part):
    count = lax.axis_size("mem")
    if count & (count - 1):
        return lax.psum(part, "mem")
    stride = 1
    while stride < count:
        part = part + lax.ppermute(part, "mem", [(i, i ^ stride) for i in range(count)])
        stride *= 2
    return part


def shifted(values, axis, step):
    zero = jnp.zeros_like(lax.slice_in_dim(values, 0, 1, axis=axis))
    if step > 0:
        return jnp.concatenate([lax.slice_in_dim(values, 1, None, axis=axis), zero], axis)
    return jnp.concatenate([zero, lax.slice_in_dim(values, 0, -1, axis=axis)], axis)


def coefficients(coef_band):
    row_coef, col_coef = coef_band[0], coef_band[1]
    row_next = shifted(shifted(row_coef, 0, -1), 0, 1)
    col_next = shifted(shifted(col_coef, 1, -1), 1, 1)
    return row_next, shifted(row_coef, 0, -1), col_next, shifted(col_coef, 1, -1)


def diffuse(values, coefs):
    row_next, row_prev, col_next, col_prev = coefs
    row_in = row_next * (shifted(values, 1, 1) - values)
    row_out = row_prev * (values - shifted(values, 1, -1))
    col_in = col_next * (shifted(values, 2, 1) - values)
    col_out = col_prev * (values - shifted(values, 2, -1))
    return values + row_in - row_out + col_in - col_out


def localize(field, coef_band):
    coefs = coefficients(coef_band)
    for repeat in range(STEPS):
        field = diffuse(field, coefs)
    return field


def per_device(controls, perturbations, jacobian, obs_weight, radar_mask, row_faces, col_faces):
    row_count = controls.shape[1]
    row_index = lax.axis_index("tile") * row_count + lax.broadcasted_iota(
        jnp.int32, row_faces.shape, 0
    )
    row_coef = jnp.where(
        row_index < row_count * lax.axis_size("tile") - 1, row_faces, jnp.zeros_like(row_faces)
    )
    stacked = jnp.stack([row_coef, col_faces])
    mix = jnp.sum(perturbations.astype(jnp.float32) * jacobian[None], axis=1)
    weights = radar_mask.astype(jnp.float32) * obs_weight
    field, coef_band = exchange([controls, stacked], 2 * STEPS)
    mix_band, weights_band = exchange([mix, weights[None]], STEPS)
    reach = row_count + 2 * STEPS
    localized = localize(field, coef_band)[:, STEPS : STEPS + reach]
    reflect = mem_sum(jnp.sum(mix_band * localized, 0))
    sensitivity = mix_band * (weights_band[0] * reflect)
    spread = localize(sensitivity, coef_band[:, STEPS : STEPS + reach])
    return controls + spread[:, STEPS : STEPS + row_count]


def solution(mesh):
    placed = (
        P("mem", "tile", None),
        P("mem", None, "tile", None),
        P(None, "tile", None),
        P("tile", None),
        P("tile", None),
        P("tile", None),
        P("tile", None),
    )
    return jax.shard_map(
        per_device, mesh=mesh, in_specs=placed, out_specs=P("mem", "tile", None), check_vma=False
    )
```

```python
import jax
import jax.numpy as jnp
from jax import lax
from jax.sharding import PartitionSpec as P

STEPS = 4


def exchange(parts, width):
    count = lax.axis_size("tile")
    cols = parts[0].shape[-1]
    sizes = [part[..., :width, :].size // cols for part in parts]
    head = jnp.concatenate([part[..., :width, :].reshape(-1, cols) for part in parts], 0)
    tail = jnp.concatenate([part[..., -width:, :].reshape(-1, cols) for part in parts], 0)
    above = lax.ppermute(tail, "tile", [(i, i + 1) for i in range(count - 1)])
    below = lax.ppermute(head, "tile", [(i + 1, i) for i in range(count - 1)])
    bands = []
    start = 0
    for part, size in zip(parts, sizes):
        shape = part.shape[:-2] + (width, cols)
        top = above[start : start + size].reshape(shape)
        bottom = below[start : start + size].reshape(shape)
        bands.append(jnp.concatenate([top, part, bottom], -2))
        start += size
    return bands


def mem_sum(part):
    count = lax.axis_size("mem")
    if count & (count - 1):
        return lax.psum(part, "mem")

    def partner(stride):
        return lax.ppermute(part, "mem", [(i, i ^ stride) for i in range(count)])

    stride = 1
    while stride < count:
        if stride * 2 < count:
            near, far, both = partner(stride), partner(2 * stride), partner(3 * stride)
            part = (part + near) + (far + both)
            stride *= 4
        else:
            part = part + partner(stride)
            stride *= 2
    return part


def diffuse(values, row_coef, col_coef):
    row_flux = row_coef[..., :-1, :] * (values[..., 1:, :] - values[..., :-1, :])
    col_flux = col_coef[..., :, :-1] * (values[..., :, 1:] - values[..., :, :-1])
    zeros_row = jnp.zeros_like(values[..., :1, :])
    zeros_col = jnp.zeros_like(values[..., :, :1])
    values = (
        values
        + jnp.concatenate([row_flux, zeros_row], -2)
        - jnp.concatenate([zeros_row, row_flux], -2)
    )
    return (
        values
        + jnp.concatenate([col_flux, zeros_col], -1)
        - jnp.concatenate([zeros_col, col_flux], -1)
    )


def localize(field, coef_band):
    for repeat in range(STEPS):
        field = diffuse(field, coef_band[0], coef_band[1])
    return field


def per_device(controls, perturbations, jacobian, obs_weight, radar_mask, row_faces, col_faces):
    row_count = controls.shape[1]
    row_index = lax.axis_index("tile") * row_count + lax.broadcasted_iota(
        jnp.int32, row_faces.shape, 0
    )
    row_coef = jnp.where(
        row_index < row_count * lax.axis_size("tile") - 1, row_faces, jnp.zeros_like(row_faces)
    )
    stacked = jnp.stack([row_coef, col_faces])
    mix = jnp.sum(perturbations.astype(jnp.float32) * jacobian[None], axis=1)
    weights = radar_mask.astype(jnp.float32) * obs_weight
    field, coef_band = exchange([controls, stacked], 2 * STEPS)
    mix_band, weights_band = exchange([mix, weights[None]], STEPS)
    reach = row_count + 2 * STEPS
    localized = localize(field, coef_band)[:, STEPS : STEPS + reach]
    reflect = mem_sum(jnp.sum(mix_band * localized, 0))
    sensitivity = mix_band * (weights_band[0] * reflect)
    spread = localize(sensitivity, coef_band[:, STEPS : STEPS + reach])
    return controls + spread[:, STEPS : STEPS + row_count]


def solution(mesh):
    placed = (
        P("mem", "tile", None),
        P("mem", None, "tile", None),
        P(None, "tile", None),
        P("tile", None),
        P("tile", None),
        P("tile", None),
        P("tile", None),
    )
    return jax.shard_map(
        per_device, mesh=mesh, in_specs=placed, out_specs=P("mem", "tile", None), check_vma=False
    )
```

```python
import jax
import jax.numpy as jnp
from jax import lax
from jax.sharding import PartitionSpec as P

STEPS = 4


def exchange(parts, width):
    count = lax.axis_size("tile")
    cols = parts[0].shape[-1]
    sizes = [part[..., :width, :].size // cols for part in parts]
    head = jnp.concatenate([part[..., :width, :].reshape(-1, cols) for part in parts], 0)
    tail = jnp.concatenate([part[..., -width:, :].reshape(-1, cols) for part in parts], 0)
    above = lax.ppermute(tail, "tile", [(i, i + 1) for i in range(count - 1)])
    below = lax.ppermute(head, "tile", [(i + 1, i) for i in range(count - 1)])
    bands = []
    start = 0
    for part, size in zip(parts, sizes):
        shape = part.shape[:-2] + (width, cols)
        top = above[start : start + size].reshape(shape)
        bottom = below[start : start + size].reshape(shape)
        bands.append(jnp.concatenate([top, part, bottom], -2))
        start += size
    return bands


def mem_sum(part):
    count = lax.axis_size("mem")
    if count & (count - 1):
        return lax.psum(part, "mem")

    def partner(stride):
        return lax.ppermute(part, "mem", [(i, i ^ stride) for i in range(count)])

    stride = 1
    while stride < count:
        if stride * 2 < count:
            near, far, both = partner(stride), partner(2 * stride), partner(3 * stride)
            part = (part + near) + (far + both)
            stride *= 4
        else:
            part = part + partner(stride)
            stride *= 2
    return part


def diffuse(values, row_coef, col_coef):
    row_flux = row_coef[..., :-1, :] * (values[..., 1:, :] - values[..., :-1, :])
    col_flux = col_coef[..., :, :-1] * (values[..., :, 1:] - values[..., :, :-1])
    zeros_row = jnp.zeros_like(values[..., :1, :])
    zeros_col = jnp.zeros_like(values[..., :, :1])
    values = (
        values
        + jnp.concatenate([row_flux, zeros_row], -2)
        - jnp.concatenate([zeros_row, row_flux], -2)
    )
    return (
        values
        + jnp.concatenate([col_flux, zeros_col], -1)
        - jnp.concatenate([zeros_col, col_flux], -1)
    )


def localize(field, coef_band):
    for repeat in range(STEPS):
        field = diffuse(field, coef_band[0], coef_band[1])
    return field


def per_device(controls, perturbations, jacobian, obs_weight, radar_mask, row_faces, col_faces):
    row_count = controls.shape[1]
    row_index = lax.axis_index("tile") * row_count + lax.broadcasted_iota(
        jnp.int32, row_faces.shape, 0
    )
    row_coef = jnp.where(
        row_index < row_count * lax.axis_size("tile") - 1, row_faces, jnp.zeros_like(row_faces)
    )
    stacked = jnp.stack([row_coef, col_faces])
    mix = jnp.sum(perturbations.astype(jnp.float32) * jacobian[None], axis=1)
    weights = radar_mask.astype(jnp.float32) * obs_weight
    field, coef_band = exchange([controls, stacked], 2 * STEPS)
    field, mix, weights = lax.optimization_barrier((field, mix, weights))
    mix_band, weights_band = exchange([mix, weights[None]], STEPS)
    reach = row_count + 2 * STEPS
    localized = localize(field, coef_band)[:, STEPS : STEPS + reach]
    reflect = mem_sum(jnp.sum(mix_band * localized, 0))
    sensitivity = mix_band * (weights_band[0] * reflect)
    spread = localize(sensitivity, coef_band[:, STEPS : STEPS + reach])
    return controls + spread[:, STEPS : STEPS + row_count]


def solution(mesh):
    placed = (
        P("mem", "tile", None),
        P("mem", None, "tile", None),
        P(None, "tile", None),
        P("tile", None),
        P("tile", None),
        P("tile", None),
        P("tile", None),
    )
    return jax.shard_map(
        per_device, mesh=mesh, in_specs=placed, out_specs=P("mem", "tile", None), check_vma=False
    )
```

```python
import jax
import jax.numpy as jnp
from jax import lax
from jax.sharding import PartitionSpec as P

STEPS = 4


def exchange(parts, width):
    count = lax.axis_size("tile")
    cols = parts[0].shape[-1]
    sizes = [part[..., :width, :].size // cols for part in parts]
    head = jnp.concatenate([part[..., :width, :].reshape(-1, cols) for part in parts], 0)
    tail = jnp.concatenate([part[..., -width:, :].reshape(-1, cols) for part in parts], 0)
    above = lax.ppermute(tail, "tile", [(i, i + 1) for i in range(count - 1)])
    below = lax.ppermute(head, "tile", [(i + 1, i) for i in range(count - 1)])
    bands = []
    start = 0
    for part, size in zip(parts, sizes):
        shape = part.shape[:-2] + (width, cols)
        top = above[start : start + size].reshape(shape)
        bottom = below[start : start + size].reshape(shape)
        bands.append(jnp.concatenate([top, part, bottom], -2))
        start += size
    return bands


def mem_sum(part):
    count = lax.axis_size("mem")
    if count & (count - 1):
        return lax.psum(part, "mem")

    def partner(stride):
        return lax.ppermute(part, "mem", [(i, i ^ stride) for i in range(count)])

    stride = 1
    while stride < count:
        if stride * 2 < count:
            near, far, both = partner(stride), partner(2 * stride), partner(3 * stride)
            part = (part + near) + (far + both)
            stride *= 4
        else:
            part = part + partner(stride)
            stride *= 2
    return part


def diffuse(values, row_coef, col_coef):
    row_flux = row_coef[..., :-1, :] * (values[..., 1:, :] - values[..., :-1, :])
    col_flux = col_coef[..., :, :-1] * (values[..., :, 1:] - values[..., :, :-1])
    zeros_row = jnp.zeros_like(values[..., :1, :])
    zeros_col = jnp.zeros_like(values[..., :, :1])
    values = (
        values
        + jnp.concatenate([row_flux, zeros_row], -2)
        - jnp.concatenate([zeros_row, row_flux], -2)
    )
    return (
        values
        + jnp.concatenate([col_flux, zeros_col], -1)
        - jnp.concatenate([zeros_col, col_flux], -1)
    )


def localize(field, coef_band):
    for repeat in range(STEPS):
        field = diffuse(field, coef_band[0], coef_band[1])
    return field


def per_device(controls, perturbations, jacobian, obs_weight, radar_mask, row_faces, col_faces):
    row_count = controls.shape[1]
    row_index = lax.axis_index("tile") * row_count + lax.broadcasted_iota(
        jnp.int32, row_faces.shape, 0
    )
    row_coef = jnp.where(
        row_index < row_count * lax.axis_size("tile") - 1, row_faces, jnp.zeros_like(row_faces)
    )
    stacked = jnp.stack([row_coef, col_faces])
    field, coef_band = exchange([controls, stacked], STEPS)
    localized = localize(field, coef_band)[:, STEPS : STEPS + row_count]
    mix = jnp.sum(perturbations.astype(jnp.float32) * jacobian[None], axis=1)
    reflect = mem_sum(jnp.sum(mix * localized, 0))
    weighted = radar_mask.astype(jnp.float32) * obs_weight * reflect
    (sensitivity,) = exchange([mix * weighted[None]], STEPS)
    return controls + localize(sensitivity, coef_band)[:, STEPS : STEPS + row_count]


def solution(mesh):
    placed = (
        P("mem", "tile", None),
        P("mem", None, "tile", None),
        P(None, "tile", None),
        P("tile", None),
        P("tile", None),
        P("tile", None),
        P("tile", None),
    )
    return jax.shard_map(
        per_device, mesh=mesh, in_specs=placed, out_specs=P("mem", "tile", None), check_vma=False
    )
```

```python
import jax
import jax.numpy as jnp
from jax import lax
from jax.sharding import PartitionSpec as P

STEPS = 4


def exchange(part, width):
    count = lax.axis_size("tile")
    head = part[..., :width, :]
    tail = part[..., -width:, :]
    above = lax.ppermute(tail, "tile", [(i, i + 1) for i in range(count - 1)])
    below = lax.ppermute(head, "tile", [(i + 1, i) for i in range(count - 1)])
    return jnp.concatenate([above, part, below], -2)


def mem_sum(part):
    count = lax.axis_size("mem")
    if count & (count - 1):
        return lax.psum(part, "mem")

    def partner(stride):
        return lax.ppermute(part, "mem", [(i, i ^ stride) for i in range(count)])

    stride = 1
    while stride < count:
        if stride * 2 < count:
            near, far, both = partner(stride), partner(2 * stride), partner(3 * stride)
            part = (part + near) + (far + both)
            stride *= 4
        else:
            part = part + partner(stride)
            stride *= 2
    return part


def diffuse(values, row_coef, col_coef):
    row_flux = row_coef[..., :-1, :] * (values[..., 1:, :] - values[..., :-1, :])
    col_flux = col_coef[..., :, :-1] * (values[..., :, 1:] - values[..., :, :-1])
    zeros_row = jnp.zeros_like(values[..., :1, :])
    zeros_col = jnp.zeros_like(values[..., :, :1])
    values = (
        values
        + jnp.concatenate([row_flux, zeros_row], -2)
        - jnp.concatenate([zeros_row, row_flux], -2)
    )
    return (
        values
        + jnp.concatenate([col_flux, zeros_col], -1)
        - jnp.concatenate([zeros_col, col_flux], -1)
    )


def localize(field, coef_band):
    for repeat in range(STEPS):
        field = diffuse(field, coef_band[0], coef_band[1])
    return field


def per_device(controls, perturbations, jacobian, obs_weight, radar_mask, row_faces, col_faces):
    row_count = controls.shape[1]
    row_index = lax.axis_index("tile") * row_count + lax.broadcasted_iota(
        jnp.int32, row_faces.shape, 0
    )
    row_coef = jnp.where(
        row_index < row_count * lax.axis_size("tile") - 1, row_faces, jnp.zeros_like(row_faces)
    )
    members = controls.shape[0]
    stacked = jnp.concatenate([controls, row_coef[None], col_faces[None]], 0)
    band = exchange(stacked, STEPS)
    field, coef_band = band[:members], band[members:]
    localized = localize(field, coef_band)[:, STEPS : STEPS + row_count]
    mix = jnp.sum(perturbations.astype(jnp.float32) * jacobian[None], axis=1)
    reflect = mem_sum(jnp.sum(mix * localized, 0))
    weighted = radar_mask.astype(jnp.float32) * obs_weight * reflect
    sensitivity = exchange(mix * weighted[None], STEPS)
    return controls + localize(sensitivity, coef_band)[:, STEPS : STEPS + row_count]


def solution(mesh):
    placed = (
        P("mem", "tile", None),
        P("mem", None, "tile", None),
        P(None, "tile", None),
        P("tile", None),
        P("tile", None),
        P("tile", None),
        P("tile", None),
    )
    return jax.shard_map(
        per_device, mesh=mesh, in_specs=placed, out_specs=P("mem", "tile", None), check_vma=False
    )
```

```python
import jax
import jax.numpy as jnp
from jax import lax
from jax.sharding import PartitionSpec as P

STEPS = 4


def exchange(part, width):
    count = lax.axis_size("tile")
    head = part[..., :width, :]
    tail = part[..., -width:, :]
    above = lax.ppermute(tail, "tile", [(i, i + 1) for i in range(count - 1)])
    below = lax.ppermute(head, "tile", [(i + 1, i) for i in range(count - 1)])
    return jnp.concatenate([above, part, below], -2)


def mem_sum(part):
    count = lax.axis_size("mem")
    rows, cols = part.shape
    if rows % count:
        return lax.psum(part, "mem")
    chunks = part.reshape(count, rows // count, cols)
    mine = jnp.sum(lax.all_to_all(chunks, "mem", 0, 0), 0)
    spread = jnp.broadcast_to(mine[None], chunks.shape)
    return lax.all_to_all(spread, "mem", 0, 0).reshape(rows, cols)


def diffuse(values, row_coef, col_coef):
    row_flux = row_coef[..., :-1, :] * (values[..., 1:, :] - values[..., :-1, :])
    col_flux = col_coef[..., :, :-1] * (values[..., :, 1:] - values[..., :, :-1])
    zeros_row = jnp.zeros_like(values[..., :1, :])
    zeros_col = jnp.zeros_like(values[..., :, :1])
    values = (
        values
        + jnp.concatenate([row_flux, zeros_row], -2)
        - jnp.concatenate([zeros_row, row_flux], -2)
    )
    return (
        values
        + jnp.concatenate([col_flux, zeros_col], -1)
        - jnp.concatenate([zeros_col, col_flux], -1)
    )


def localize(field, coef_band):
    for repeat in range(STEPS):
        field = diffuse(field, coef_band[0], coef_band[1])
    return field


def per_device(controls, perturbations, jacobian, obs_weight, radar_mask, row_faces, col_faces):
    row_count = controls.shape[1]
    row_index = lax.axis_index("tile") * row_count + lax.broadcasted_iota(
        jnp.int32, row_faces.shape, 0
    )
    row_coef = jnp.where(
        row_index < row_count * lax.axis_size("tile") - 1, row_faces, jnp.zeros_like(row_faces)
    )
    members = controls.shape[0]
    stacked = jnp.concatenate([controls, row_coef[None], col_faces[None]], 0)
    band = exchange(stacked, STEPS)
    field, coef_band = band[:members], band[members:]
    localized = localize(field, coef_band)[:, STEPS : STEPS + row_count]
    mix = jnp.sum(perturbations.astype(jnp.float32) * jacobian[None], axis=1)
    reflect = mem_sum(jnp.sum(mix * localized, 0))
    weighted = radar_mask.astype(jnp.float32) * obs_weight * reflect
    sensitivity = exchange(mix * weighted[None], STEPS)
    return controls + localize(sensitivity, coef_band)[:, STEPS : STEPS + row_count]


def solution(mesh):
    placed = (
        P("mem", "tile", None),
        P("mem", None, "tile", None),
        P(None, "tile", None),
        P("tile", None),
        P("tile", None),
        P("tile", None),
        P("tile", None),
    )
    return jax.shard_map(
        per_device, mesh=mesh, in_specs=placed, out_specs=P("mem", "tile", None), check_vma=False
    )
```

```python
import jax
import jax.numpy as jnp
from jax import lax
from jax.sharding import PartitionSpec as P

STEPS = 4


def exchange(part, width):
    count = lax.axis_size("tile")
    head = part[..., :width, :]
    tail = part[..., -width:, :]
    if count % 2:
        above = lax.ppermute(tail, "tile", [(i, i + 1) for i in range(count - 1)])
        below = lax.ppermute(head, "tile", [(i + 1, i) for i in range(count - 1)])
        return jnp.concatenate([above, part, below], -2)
    odd = lax.axis_index("tile") % 2 == 1
    pairs = lambda first: [(i, i + 1) for i in range(first, count - 1, 2)] + [
        (i + 1, i) for i in range(first, count - 1, 2)
    ]
    far = lax.ppermute(jnp.where(odd, tail, head), "tile", pairs(1))
    near = lax.ppermute(jnp.where(odd, head, tail), "tile", pairs(0))
    above = jnp.where(odd, near, far)
    below = jnp.where(odd, far, near)
    return jnp.concatenate([above, part, below], -2)


def mem_sum(part):
    count = lax.axis_size("mem")
    if count & (count - 1):
        return lax.psum(part, "mem")

    def partner(stride):
        return lax.ppermute(part, "mem", [(i, i ^ stride) for i in range(count)])

    stride = 1
    while stride < count:
        if stride * 2 < count:
            near, far, both = partner(stride), partner(2 * stride), partner(3 * stride)
            part = (part + near) + (far + both)
            stride *= 4
        else:
            part = part + partner(stride)
            stride *= 2
    return part


def diffuse(values, row_coef, col_coef):
    row_flux = row_coef[..., :-1, :] * (values[..., 1:, :] - values[..., :-1, :])
    col_flux = col_coef[..., :, :-1] * (values[..., :, 1:] - values[..., :, :-1])
    zeros_row = jnp.zeros_like(values[..., :1, :])
    zeros_col = jnp.zeros_like(values[..., :, :1])
    values = (
        values
        + jnp.concatenate([row_flux, zeros_row], -2)
        - jnp.concatenate([zeros_row, row_flux], -2)
    )
    return (
        values
        + jnp.concatenate([col_flux, zeros_col], -1)
        - jnp.concatenate([zeros_col, col_flux], -1)
    )


def localize(field, coef_band):
    for repeat in range(STEPS):
        field = diffuse(field, coef_band[0], coef_band[1])
    return field


def per_device(controls, perturbations, jacobian, obs_weight, radar_mask, row_faces, col_faces):
    row_count = controls.shape[1]
    row_index = lax.axis_index("tile") * row_count + lax.broadcasted_iota(
        jnp.int32, row_faces.shape, 0
    )
    row_coef = jnp.where(
        row_index < row_count * lax.axis_size("tile") - 1, row_faces, jnp.zeros_like(row_faces)
    )
    members = controls.shape[0]
    stacked = jnp.concatenate([controls, row_coef[None], col_faces[None]], 0)
    band = exchange(stacked, STEPS)
    field, coef_band = band[:members], band[members:]
    localized = localize(field, coef_band)[:, STEPS : STEPS + row_count]
    mix = jnp.sum(perturbations.astype(jnp.float32) * jacobian[None], axis=1)
    reflect = mem_sum(jnp.sum(mix * localized, 0))
    weighted = radar_mask.astype(jnp.float32) * obs_weight * reflect
    sensitivity = exchange(mix * weighted[None], STEPS)
    return controls + localize(sensitivity, coef_band)[:, STEPS : STEPS + row_count]


def solution(mesh):
    placed = (
        P("mem", "tile", None),
        P("mem", None, "tile", None),
        P(None, "tile", None),
        P("tile", None),
        P("tile", None),
        P("tile", None),
        P("tile", None),
    )
    return jax.shard_map(
        per_device, mesh=mesh, in_specs=placed, out_specs=P("mem", "tile", None), check_vma=False
    )
```

```python
import jax
import jax.numpy as jnp
from jax import lax
from jax.sharding import PartitionSpec as P

STEPS = 4


def exchange(part, width):
    count = lax.axis_size("tile")
    head = part[..., :width, :]
    tail = part[..., -width:, :]
    if count % 2:
        above = lax.ppermute(tail, "tile", [(i, i + 1) for i in range(count - 1)])
        below = lax.ppermute(head, "tile", [(i + 1, i) for i in range(count - 1)])
        return jnp.concatenate([above, part, below], -2)
    odd = lax.axis_index("tile") % 2 == 1
    pairs = lambda first: [(i, i + 1) for i in range(first, count - 1, 2)] + [
        (i + 1, i) for i in range(first, count - 1, 2)
    ]
    far = lax.ppermute(jnp.where(odd, tail, head), "tile", pairs(1))
    near = lax.ppermute(jnp.where(odd, head, tail), "tile", pairs(0))
    above = jnp.where(odd, near, far)
    below = jnp.where(odd, far, near)
    return jnp.concatenate([above, part, below], -2)


def mem_sum(part):
    count = lax.axis_size("mem")
    if count & (count - 1):
        return lax.psum(part, "mem")

    def partner(stride):
        return lax.ppermute(part, "mem", [(i, i ^ stride) for i in range(count)])

    stride = 1
    while stride < count:
        if stride * 2 < count:
            near, far, both = partner(stride), partner(2 * stride), partner(3 * stride)
            part = (part + near) + (far + both)
            stride *= 4
        else:
            part = part + partner(stride)
            stride *= 2
    return part


def diffuse(values, row_coef, col_coef):
    row_flux = row_coef[..., :-1, :] * (values[..., 1:, :] - values[..., :-1, :])
    col_flux = col_coef[..., :, :-1] * (values[..., :, 1:] - values[..., :, :-1])
    zeros_row = jnp.zeros_like(values[..., :1, :])
    zeros_col = jnp.zeros_like(values[..., :, :1])
    values = (
        values
        + jnp.concatenate([row_flux, zeros_row], -2)
        - jnp.concatenate([zeros_row, row_flux], -2)
    )
    return (
        values
        + jnp.concatenate([col_flux, zeros_col], -1)
        - jnp.concatenate([zeros_col, col_flux], -1)
    )


def localize(field, coef_band):
    for repeat in range(STEPS):
        field = diffuse(field, coef_band[0], coef_band[1])
    return field


def per_device(controls, perturbations, jacobian, obs_weight, radar_mask, row_faces, col_faces):
    members, row_count = controls.shape[:2]
    row_index = lax.axis_index("tile") * row_count + lax.broadcasted_iota(
        jnp.int32, row_faces.shape, 0
    )
    row_coef = jnp.where(
        row_index < row_count * lax.axis_size("tile") - 1, row_faces, jnp.zeros_like(row_faces)
    )
    mix = jnp.sum(perturbations.astype(jnp.float32) * jacobian[None], axis=1)
    stacked = jnp.concatenate([controls, row_coef[None], col_faces[None], mix], 0)
    band = exchange(stacked, STEPS)
    field, coef_band, mix_band = band[:members], band[members : members + 2], band[members + 2 :]
    localized = localize(field, coef_band)[:, STEPS : STEPS + row_count]
    reflect = mem_sum(jnp.sum(mix * localized, 0))
    weighted = radar_mask.astype(jnp.float32) * obs_weight * reflect
    weighted_band = exchange(weighted[None], STEPS)
    sensitivity = mix_band * weighted_band
    return controls + localize(sensitivity, coef_band)[:, STEPS : STEPS + row_count]


def solution(mesh):
    placed = (
        P("mem", "tile", None),
        P("mem", None, "tile", None),
        P(None, "tile", None),
        P("tile", None),
        P("tile", None),
        P("tile", None),
        P("tile", None),
    )
    return jax.shard_map(
        per_device, mesh=mesh, in_specs=placed, out_specs=P("mem", "tile", None), check_vma=False
    )
```

```python
import jax
import jax.numpy as jnp
from jax import lax
from jax.sharding import PartitionSpec as P

STEPS = 4


def exchange(part, width):
    count = lax.axis_size("tile")
    head = part[..., :width, :]
    tail = part[..., -width:, :]
    if count % 2:
        above = lax.ppermute(tail, "tile", [(i, i + 1) for i in range(count - 1)])
        below = lax.ppermute(head, "tile", [(i + 1, i) for i in range(count - 1)])
        return jnp.concatenate([above, part, below], -2)
    odd = lax.axis_index("tile") % 2 == 1
    pairs = lambda first: [(i, i + 1) for i in range(first, count - 1, 2)] + [
        (i + 1, i) for i in range(first, count - 1, 2)
    ]
    far = lax.ppermute(jnp.where(odd, tail, head), "tile", pairs(1))
    near = lax.ppermute(jnp.where(odd, head, tail), "tile", pairs(0))
    above = jnp.where(odd, near, far)
    below = jnp.where(odd, far, near)
    return jnp.concatenate([above, part, below], -2)


def split_exchange(part, width):
    count = lax.axis_size("tile")
    head = part[..., :width, :]
    tail = part[..., -width:, :]
    zero = jnp.zeros_like(head)
    if count % 2:
        band = exchange(part, width)
        return band, zero, False
    odd = lax.axis_index("tile") % 2 == 1
    pairs = lambda first: [(i, i + 1) for i in range(first, count - 1, 2)] + [
        (i + 1, i) for i in range(first, count - 1, 2)
    ]
    far = lax.ppermute(jnp.where(odd, tail, head), "tile", pairs(1))
    near = lax.ppermute(jnp.where(odd, head, tail), "tile", pairs(0))
    above = jnp.where(odd, near, zero)
    below = jnp.where(odd, zero, near)
    return jnp.concatenate([above, part, below], -2), far, odd


def mem_sum(part):
    count = lax.axis_size("mem")
    if count & (count - 1):
        return lax.psum(part, "mem")

    def partner(stride):
        return lax.ppermute(part, "mem", [(i, i ^ stride) for i in range(count)])

    stride = 1
    while stride < count:
        if stride * 2 < count:
            near, far, both = partner(stride), partner(2 * stride), partner(3 * stride)
            part = (part + near) + (far + both)
            stride *= 4
        else:
            part = part + partner(stride)
            stride *= 2
    return part


def diffuse(values, row_coef, col_coef):
    row_flux = row_coef[..., :-1, :] * (values[..., 1:, :] - values[..., :-1, :])
    col_flux = col_coef[..., :, :-1] * (values[..., :, 1:] - values[..., :, :-1])
    zeros_row = jnp.zeros_like(values[..., :1, :])
    zeros_col = jnp.zeros_like(values[..., :, :1])
    values = (
        values
        + jnp.concatenate([row_flux, zeros_row], -2)
        - jnp.concatenate([zeros_row, row_flux], -2)
    )
    return (
        values
        + jnp.concatenate([col_flux, zeros_col], -1)
        - jnp.concatenate([zeros_col, col_flux], -1)
    )


def localize(field, coef_band):
    for repeat in range(STEPS):
        field = diffuse(field, coef_band[0], coef_band[1])
    return field


def per_device(controls, perturbations, jacobian, obs_weight, radar_mask, row_faces, col_faces):
    row_count = controls.shape[1]
    row_index = lax.axis_index("tile") * row_count + lax.broadcasted_iota(
        jnp.int32, row_faces.shape, 0
    )
    row_coef = jnp.where(
        row_index < row_count * lax.axis_size("tile") - 1, row_faces, jnp.zeros_like(row_faces)
    )
    members = controls.shape[0]
    stacked = jnp.concatenate([controls, row_coef[None], col_faces[None]], 0)
    band = exchange(stacked, STEPS)
    field, coef_band = band[:members], band[members:]
    localized = localize(field, coef_band)[:, STEPS : STEPS + row_count]
    mix = jnp.sum(perturbations.astype(jnp.float32) * jacobian[None], axis=1)
    reflect = mem_sum(jnp.sum(mix * localized, 0))
    weighted = radar_mask.astype(jnp.float32) * obs_weight * reflect
    sensitivity, far, odd = split_exchange(mix * weighted[None], STEPS)
    spread = localize(sensitivity, coef_band)[:, STEPS : STEPS + row_count]
    spread, far = lax.optimization_barrier((spread, far))
    zero = jnp.zeros_like(far)
    strip = jnp.where(odd, jnp.concatenate([zero, far], 1), jnp.concatenate([far, zero], 1))
    strip_coef = jnp.where(odd, coef_band[:, row_count:], coef_band[:, : 2 * STEPS])
    edge = localize(strip, strip_coef)
    rest = jnp.zeros_like(spread[:, STEPS:])
    edge = jnp.where(
        odd,
        jnp.concatenate([rest, edge[:, :STEPS]], 1),
        jnp.concatenate([edge[:, STEPS:], rest], 1),
    )
    return controls + (spread + edge)


def solution(mesh):
    placed = (
        P("mem", "tile", None),
        P("mem", None, "tile", None),
        P(None, "tile", None),
        P("tile", None),
        P("tile", None),
        P("tile", None),
        P("tile", None),
    )
    return jax.shard_map(
        per_device, mesh=mesh, in_specs=placed, out_specs=P("mem", "tile", None), check_vma=False
    )
```

```python
import jax
import jax.numpy as jnp
from jax import lax
from jax.sharding import PartitionSpec as P

STEPS = 4


def exchange(part, width):
    count = lax.axis_size("tile")
    head = part[..., :width, :]
    tail = part[..., -width:, :]
    if count % 2:
        above = lax.ppermute(tail, "tile", [(i, i + 1) for i in range(count - 1)])
        below = lax.ppermute(head, "tile", [(i + 1, i) for i in range(count - 1)])
        return jnp.concatenate([above, part, below], -2)
    odd = lax.axis_index("tile") % 2 == 1
    pairs = lambda first: [(i, i + 1) for i in range(first, count - 1, 2)] + [
        (i + 1, i) for i in range(first, count - 1, 2)
    ]
    far = lax.ppermute(jnp.where(odd, tail, head), "tile", pairs(1))
    near = lax.ppermute(jnp.where(odd, head, tail), "tile", pairs(0))
    above = jnp.where(odd, near, far)
    below = jnp.where(odd, far, near)
    return jnp.concatenate([above, part, below], -2)


def tile_pairs(first):
    count = lax.axis_size("tile")
    return [(i, i + 1) for i in range(first, count - 1, 2)] + [
        (i + 1, i) for i in range(first, count - 1, 2)
    ]


def mem_sum(part):
    count = lax.axis_size("mem")
    if count & (count - 1):
        return lax.psum(part, "mem")

    def partner(stride):
        return lax.ppermute(part, "mem", [(i, i ^ stride) for i in range(count)])

    stride = 1
    while stride < count:
        if stride * 2 < count:
            near, far, both = partner(stride), partner(2 * stride), partner(3 * stride)
            part = (part + near) + (far + both)
            stride *= 4
        else:
            part = part + partner(stride)
            stride *= 2
    return part


def diffuse(values, row_coef, col_coef):
    row_flux = row_coef[..., :-1, :] * (values[..., 1:, :] - values[..., :-1, :])
    col_flux = col_coef[..., :, :-1] * (values[..., :, 1:] - values[..., :, :-1])
    zeros_row = jnp.zeros_like(values[..., :1, :])
    zeros_col = jnp.zeros_like(values[..., :, :1])
    values = (
        values
        + jnp.concatenate([row_flux, zeros_row], -2)
        - jnp.concatenate([zeros_row, row_flux], -2)
    )
    return (
        values
        + jnp.concatenate([col_flux, zeros_col], -1)
        - jnp.concatenate([zeros_col, col_flux], -1)
    )


def localize(field, coef_band):
    for repeat in range(STEPS):
        field = diffuse(field, coef_band[0], coef_band[1])
    return field


def per_device(controls, perturbations, jacobian, obs_weight, radar_mask, row_faces, col_faces):
    row_count = controls.shape[1]
    row_index = lax.axis_index("tile") * row_count + lax.broadcasted_iota(
        jnp.int32, row_faces.shape, 0
    )
    row_coef = jnp.where(
        row_index < row_count * lax.axis_size("tile") - 1, row_faces, jnp.zeros_like(row_faces)
    )
    members = controls.shape[0]
    stacked = jnp.concatenate([controls, row_coef[None], col_faces[None]], 0)
    band = exchange(stacked, STEPS)
    field, coef_band = band[:members], band[members:]
    localized = localize(field, coef_band)[:, STEPS : STEPS + row_count]
    mix = jnp.sum(perturbations.astype(jnp.float32) * jacobian[None], axis=1)
    reflect = mem_sum(jnp.sum(mix * localized, 0))
    weighted = radar_mask.astype(jnp.float32) * obs_weight * reflect
    sensitivity = mix * weighted[None]
    head = sensitivity[:, :STEPS]
    tail = sensitivity[:, -STEPS:]
    zero = jnp.zeros_like(head)
    if lax.axis_size("tile") % 2:
        spread = localize(exchange(sensitivity, STEPS), coef_band)[:, STEPS : STEPS + row_count]
        return controls + spread
    odd = lax.axis_index("tile") % 2 == 1
    near = lax.ppermute(jnp.where(odd, head, tail), "tile", tile_pairs(0))
    band = jnp.concatenate([jnp.where(odd, near, zero), sensitivity, jnp.where(odd, zero, near)], 1)
    spread = localize(band, coef_band)[:, STEPS : STEPS + row_count]
    spread, outgoing = lax.optimization_barrier((spread, jnp.where(odd, tail, head)))
    far = lax.ppermute(outgoing, "tile", tile_pairs(1))
    zero = jnp.zeros_like(far)
    strip = jnp.where(odd, jnp.concatenate([zero, far], 1), jnp.concatenate([far, zero], 1))
    strip_coef = jnp.where(odd, coef_band[:, row_count:], coef_band[:, : 2 * STEPS])
    edge = localize(strip, strip_coef)
    rest = jnp.zeros_like(spread[:, STEPS:])
    edge = jnp.where(
        odd,
        jnp.concatenate([rest, edge[:, :STEPS]], 1),
        jnp.concatenate([edge[:, STEPS:], rest], 1),
    )
    return controls + (spread + edge)


def solution(mesh):
    placed = (
        P("mem", "tile", None),
        P("mem", None, "tile", None),
        P(None, "tile", None),
        P("tile", None),
        P("tile", None),
        P("tile", None),
        P("tile", None),
    )
    return jax.shard_map(
        per_device, mesh=mesh, in_specs=placed, out_specs=P("mem", "tile", None), check_vma=False
    )
```

```python
import jax
import jax.numpy as jnp
from jax import lax
from jax.sharding import PartitionSpec as P

STEPS = 4


def exchange(part, width):
    count = lax.axis_size("tile")
    head = part[..., :width, :]
    tail = part[..., -width:, :]
    if count % 2:
        above = lax.ppermute(tail, "tile", [(i, i + 1) for i in range(count - 1)])
        below = lax.ppermute(head, "tile", [(i + 1, i) for i in range(count - 1)])
        return jnp.concatenate([above, part, below], -2)
    odd = lax.axis_index("tile") % 2 == 1
    pairs = lambda first: [(i, i + 1) for i in range(first, count - 1, 2)] + [
        (i + 1, i) for i in range(first, count - 1, 2)
    ]
    far = lax.ppermute(jnp.where(odd, tail, head), "tile", pairs(1))
    near = lax.ppermute(jnp.where(odd, head, tail), "tile", pairs(0))
    above = jnp.where(odd, near, far)
    below = jnp.where(odd, far, near)
    return jnp.concatenate([above, part, below], -2)


def split_exchange(part, width):
    count = lax.axis_size("tile")
    head = part[..., :width, :]
    tail = part[..., -width:, :]
    odd = lax.axis_index("tile") % 2 == 1
    pairs = lambda first: [(i, i + 1) for i in range(first, count - 1, 2)] + [
        (i + 1, i) for i in range(first, count - 1, 2)
    ]
    far = lax.ppermute(jnp.where(odd, tail, head), "tile", pairs(1))
    near = lax.ppermute(jnp.where(odd, head, tail), "tile", pairs(0))
    return near, far, odd


def near_band(part, near, odd):
    zero = jnp.zeros_like(near)
    return jnp.concatenate([jnp.where(odd, near, zero), part, jnp.where(odd, zero, near)], -2)


def full_band(part, near, far, odd):
    return jnp.concatenate([jnp.where(odd, near, far), part, jnp.where(odd, far, near)], -2)


def mem_sum(part):
    count = lax.axis_size("mem")
    if count & (count - 1):
        return lax.psum(part, "mem")

    def partner(stride):
        return lax.ppermute(part, "mem", [(i, i ^ stride) for i in range(count)])

    stride = 1
    while stride < count:
        if stride * 2 < count:
            near, far, both = partner(stride), partner(2 * stride), partner(3 * stride)
            part = (part + near) + (far + both)
            stride *= 4
        else:
            part = part + partner(stride)
            stride *= 2
    return part


def diffuse(values, row_coef, col_coef):
    row_flux = row_coef[..., :-1, :] * (values[..., 1:, :] - values[..., :-1, :])
    col_flux = col_coef[..., :, :-1] * (values[..., :, 1:] - values[..., :, :-1])
    zeros_row = jnp.zeros_like(values[..., :1, :])
    zeros_col = jnp.zeros_like(values[..., :, :1])
    values = (
        values
        + jnp.concatenate([row_flux, zeros_row], -2)
        - jnp.concatenate([zeros_row, row_flux], -2)
    )
    return (
        values
        + jnp.concatenate([col_flux, zeros_col], -1)
        - jnp.concatenate([zeros_col, col_flux], -1)
    )


def localize(field, coef_band):
    for repeat in range(STEPS):
        field = diffuse(field, coef_band[0], coef_band[1])
    return field


def per_device(controls, perturbations, jacobian, obs_weight, radar_mask, row_faces, col_faces):
    members, row_count = controls.shape[:2]
    row_index = lax.axis_index("tile") * row_count + lax.broadcasted_iota(
        jnp.int32, row_faces.shape, 0
    )
    row_coef = jnp.where(
        row_index < row_count * lax.axis_size("tile") - 1, row_faces, jnp.zeros_like(row_faces)
    )
    mix = jnp.sum(perturbations.astype(jnp.float32) * jacobian[None], axis=1)
    stacked = jnp.concatenate([controls, row_coef[None], col_faces[None]], 0)
    if lax.axis_size("tile") % 2:
        band = exchange(stacked, STEPS)
        field, coef_band = band[:members], band[members:]
        localized = localize(field, coef_band)[:, STEPS : STEPS + row_count]
        reflect = mem_sum(jnp.sum(mix * localized, 0))
        weighted = radar_mask.astype(jnp.float32) * obs_weight * reflect
        sensitivity = exchange(mix * weighted[None], STEPS)
        return controls + localize(sensitivity, coef_band)[:, STEPS : STEPS + row_count]
    near, far, odd = split_exchange(stacked, STEPS)
    partial = near_band(stacked, near, odd)
    main = localize(partial[:members], partial[members:])[:, STEPS : STEPS + row_count]
    main, far = lax.optimization_barrier((main, far))
    band = full_band(stacked, near, far, odd)
    coef_band = band[members:]
    strip = jnp.where(odd, band[:, row_count - STEPS :], band[:, : 3 * STEPS])
    edge = localize(strip[:members], strip[members:])[:, STEPS : 2 * STEPS]
    localized = jnp.where(
        odd,
        jnp.concatenate([main[:, : row_count - STEPS], edge], 1),
        jnp.concatenate([edge, main[:, STEPS:]], 1),
    )
    reflect = mem_sum(jnp.sum(mix * localized, 0))
    weighted = radar_mask.astype(jnp.float32) * obs_weight * reflect
    near, far, odd = split_exchange(mix * weighted[None], STEPS)
    spread = localize(near_band(mix * weighted[None], near, odd), coef_band)
    spread = spread[:, STEPS : STEPS + row_count]
    spread, far = lax.optimization_barrier((spread, far))
    zero = jnp.zeros_like(far)
    strip = jnp.where(odd, jnp.concatenate([zero, far], 1), jnp.concatenate([far, zero], 1))
    strip_coef = jnp.where(odd, coef_band[:, row_count:], coef_band[:, : 2 * STEPS])
    edge = localize(strip, strip_coef)
    rest = jnp.zeros_like(spread[:, STEPS:])
    edge = jnp.where(
        odd,
        jnp.concatenate([rest, edge[:, :STEPS]], 1),
        jnp.concatenate([edge[:, STEPS:], rest], 1),
    )
    return controls + (spread + edge)


def solution(mesh):
    placed = (
        P("mem", "tile", None),
        P("mem", None, "tile", None),
        P(None, "tile", None),
        P("tile", None),
        P("tile", None),
        P("tile", None),
        P("tile", None),
    )
    return jax.shard_map(
        per_device, mesh=mesh, in_specs=placed, out_specs=P("mem", "tile", None), check_vma=False
    )
```

```python
import jax
import jax.numpy as jnp
from jax import lax
from jax.sharding import PartitionSpec as P

STEPS = 4


def exchange(part, width):
    count = lax.axis_size("tile")
    head = part[..., :width, :]
    tail = part[..., -width:, :]
    if count % 2:
        above = lax.ppermute(tail, "tile", [(i, i + 1) for i in range(count - 1)])
        below = lax.ppermute(head, "tile", [(i + 1, i) for i in range(count - 1)])
        return jnp.concatenate([above, part, below], -2)
    odd = lax.axis_index("tile") % 2 == 1
    pairs = lambda first: [(i, i + 1) for i in range(first, count - 1, 2)] + [
        (i + 1, i) for i in range(first, count - 1, 2)
    ]
    far = lax.ppermute(jnp.where(odd, tail, head), "tile", pairs(1))
    near = lax.ppermute(jnp.where(odd, head, tail), "tile", pairs(0))
    above = jnp.where(odd, near, far)
    below = jnp.where(odd, far, near)
    return jnp.concatenate([above, part, below], -2)


def split_exchange(part, width):
    count = lax.axis_size("tile")
    rows = part.shape[-2]
    odd = lax.axis_index("tile") % 2 == 1
    pairs = lambda first: [(i, i + 1) for i in range(first, count - 1, 2)] + [
        (i + 1, i) for i in range(first, count - 1, 2)
    ]
    far_start = jnp.where(odd, rows - width, 0)
    near_start = jnp.where(odd, 0, rows - width)
    outgoing = lax.dynamic_slice_in_dim(part, far_start, width, axis=part.ndim - 2)
    far = lax.ppermute(outgoing, "tile", pairs(1))
    outgoing = lax.dynamic_slice_in_dim(part, near_start, width, axis=part.ndim - 2)
    near = lax.ppermute(outgoing, "tile", pairs(0))
    return near, far, odd


def near_band(part, near, odd):
    zero = jnp.zeros_like(near)
    return jnp.concatenate([jnp.where(odd, near, zero), part, jnp.where(odd, zero, near)], -2)


def full_band(part, near, far, odd):
    return jnp.concatenate([jnp.where(odd, near, far), part, jnp.where(odd, far, near)], -2)


def mem_sum(part):
    count = lax.axis_size("mem")
    if count & (count - 1):
        return lax.psum(part, "mem")

    def partner(stride):
        return lax.ppermute(part, "mem", [(i, i ^ stride) for i in range(count)])

    stride = 1
    while stride < count:
        if stride * 2 < count:
            near, far, both = partner(stride), partner(2 * stride), partner(3 * stride)
            part = (part + near) + (far + both)
            stride *= 4
        else:
            part = part + partner(stride)
            stride *= 2
    return part


def diffuse(values, row_coef, col_coef):
    row_flux = row_coef[..., :-1, :] * (values[..., 1:, :] - values[..., :-1, :])
    col_flux = col_coef[..., :, :-1] * (values[..., :, 1:] - values[..., :, :-1])
    zeros_row = jnp.zeros_like(values[..., :1, :])
    zeros_col = jnp.zeros_like(values[..., :, :1])
    values = (
        values
        + jnp.concatenate([row_flux, zeros_row], -2)
        - jnp.concatenate([zeros_row, row_flux], -2)
    )
    return (
        values
        + jnp.concatenate([col_flux, zeros_col], -1)
        - jnp.concatenate([zeros_col, col_flux], -1)
    )


def localize(field, coef_band):
    for repeat in range(STEPS):
        field = diffuse(field, coef_band[0], coef_band[1])
    return field


def per_device(controls, perturbations, jacobian, obs_weight, radar_mask, row_faces, col_faces):
    members, row_count = controls.shape[:2]
    last_row = row_count * lax.axis_size("tile") - 1 - lax.axis_index("tile") * row_count

    def masked(coefs, first):
        band_row = first + lax.broadcasted_iota(jnp.int32, coefs.shape, 1)
        keep = (band_row != last_row) | (lax.broadcasted_iota(jnp.int32, coefs.shape, 0) > 0)
        return jnp.where(keep, coefs, jnp.zeros_like(coefs))

    row_coef = row_faces
    mix = jnp.sum(perturbations.astype(jnp.float32) * jacobian[None], axis=1)
    stacked = jnp.concatenate([controls, row_coef[None], col_faces[None]], 0)
    if lax.axis_size("tile") % 2:
        band = exchange(stacked, STEPS)
        field, coef_band = band[:members], masked(band[members:], -STEPS)
        localized = localize(field, coef_band)[:, STEPS : STEPS + row_count]
        reflect = mem_sum(jnp.sum(mix * localized, 0))
        weighted = radar_mask.astype(jnp.float32) * obs_weight * reflect
        sensitivity = exchange(mix * weighted[None], STEPS)
        return controls + localize(sensitivity, coef_band)[:, STEPS : STEPS + row_count]
    near, far, odd = split_exchange(stacked, STEPS)
    partial = near_band(stacked, near, odd)
    main = localize(partial[:members], masked(partial[members:], -STEPS))
    main = main[:, STEPS : STEPS + row_count]
    main, far = lax.optimization_barrier((main, far))
    band = full_band(stacked, near, far, odd)
    band = jnp.concatenate([band[:members], masked(band[members:], -STEPS)], 0)
    coef_band = band[members:]
    strip = jnp.where(odd, band[:, row_count - STEPS :], band[:, : 3 * STEPS])
    edge = localize(strip[:members], strip[members:])[:, STEPS : 2 * STEPS]
    localized = jnp.where(
        odd,
        jnp.concatenate([main[:, : row_count - STEPS], edge], 1),
        jnp.concatenate([edge, main[:, STEPS:]], 1),
    )
    reflect = mem_sum(jnp.sum(mix * localized, 0))
    weighted = radar_mask.astype(jnp.float32) * obs_weight * reflect
    near, far, odd = split_exchange(mix * weighted[None], STEPS)
    spread = localize(near_band(mix * weighted[None], near, odd), coef_band)
    spread = spread[:, STEPS : STEPS + row_count]
    spread, far = lax.optimization_barrier((spread, far))
    zero = jnp.zeros_like(far)
    strip = jnp.where(odd, jnp.concatenate([zero, far], 1), jnp.concatenate([far, zero], 1))
    strip_coef = jnp.where(odd, coef_band[:, row_count:], coef_band[:, : 2 * STEPS])
    edge = localize(strip, strip_coef)
    rest = jnp.zeros_like(spread[:, STEPS:])
    edge = jnp.where(
        odd,
        jnp.concatenate([rest, edge[:, :STEPS]], 1),
        jnp.concatenate([edge[:, STEPS:], rest], 1),
    )
    return controls + (spread + edge)


def solution(mesh):
    placed = (
        P("mem", "tile", None),
        P("mem", None, "tile", None),
        P(None, "tile", None),
        P("tile", None),
        P("tile", None),
        P("tile", None),
        P("tile", None),
    )
    return jax.shard_map(
        per_device, mesh=mesh, in_specs=placed, out_specs=P("mem", "tile", None), check_vma=False
    )
```

```python
import jax
import jax.numpy as jnp
from jax import lax
from jax.sharding import PartitionSpec as P

STEPS = 4


def exchange(part, width):
    count = lax.axis_size("tile")
    head = part[..., :width, :]
    tail = part[..., -width:, :]
    if count % 2:
        above = lax.ppermute(tail, "tile", [(i, i + 1) for i in range(count - 1)])
        below = lax.ppermute(head, "tile", [(i + 1, i) for i in range(count - 1)])
        return jnp.concatenate([above, part, below], -2)
    odd = lax.axis_index("tile") % 2 == 1
    pairs = lambda first: [(i, i + 1) for i in range(first, count - 1, 2)] + [
        (i + 1, i) for i in range(first, count - 1, 2)
    ]
    far = lax.ppermute(jnp.where(odd, tail, head), "tile", pairs(1))
    far, outgoing = lax.optimization_barrier((far, jnp.where(odd, head, tail)))
    near = lax.ppermute(outgoing, "tile", pairs(0))
    above = jnp.where(odd, near, far)
    below = jnp.where(odd, far, near)
    return jnp.concatenate([above, part, below], -2)


def mem_sum(part):
    count = lax.axis_size("mem")
    if count & (count - 1):
        return lax.psum(part, "mem")

    def partner(stride):
        return lax.ppermute(part, "mem", [(i, i ^ stride) for i in range(count)])

    stride = 1
    while stride < count:
        if stride * 2 < count:
            near, far, both = partner(stride), partner(2 * stride), partner(3 * stride)
            part = (part + near) + (far + both)
            stride *= 4
        else:
            part = part + partner(stride)
            stride *= 2
    return part


def diffuse(values, row_coef, col_coef):
    row_flux = row_coef[..., :-1, :] * (values[..., 1:, :] - values[..., :-1, :])
    col_flux = col_coef[..., :, :-1] * (values[..., :, 1:] - values[..., :, :-1])
    zeros_row = jnp.zeros_like(values[..., :1, :])
    zeros_col = jnp.zeros_like(values[..., :, :1])
    values = (
        values
        + jnp.concatenate([row_flux, zeros_row], -2)
        - jnp.concatenate([zeros_row, row_flux], -2)
    )
    return (
        values
        + jnp.concatenate([col_flux, zeros_col], -1)
        - jnp.concatenate([zeros_col, col_flux], -1)
    )


def localize(field, coef_band):
    for repeat in range(STEPS):
        field = diffuse(field, coef_band[0], coef_band[1])
    return field


def per_device(controls, perturbations, jacobian, obs_weight, radar_mask, row_faces, col_faces):
    row_count = controls.shape[1]
    row_index = lax.axis_index("tile") * row_count + lax.broadcasted_iota(
        jnp.int32, row_faces.shape, 0
    )
    row_coef = jnp.where(
        row_index < row_count * lax.axis_size("tile") - 1, row_faces, jnp.zeros_like(row_faces)
    )
    members = controls.shape[0]
    stacked = jnp.concatenate([controls, row_coef[None], col_faces[None]], 0)
    band = exchange(stacked, STEPS)
    field, coef_band = band[:members], band[members:]
    localized = localize(field, coef_band)[:, STEPS : STEPS + row_count]
    mix = jnp.sum(perturbations.astype(jnp.float32) * jacobian[None], axis=1)
    reflect = mem_sum(jnp.sum(mix * localized, 0))
    weighted = radar_mask.astype(jnp.float32) * obs_weight * reflect
    sensitivity = exchange(mix * weighted[None], STEPS)
    return controls + localize(sensitivity, coef_band)[:, STEPS : STEPS + row_count]


def solution(mesh):
    placed = (
        P("mem", "tile", None),
        P("mem", None, "tile", None),
        P(None, "tile", None),
        P("tile", None),
        P("tile", None),
        P("tile", None),
        P("tile", None),
    )
    return jax.shard_map(
        per_device, mesh=mesh, in_specs=placed, out_specs=P("mem", "tile", None), check_vma=False
    )
```

```python
import jax
import jax.numpy as jnp
from jax import lax
from jax.sharding import PartitionSpec as P

STEPS = 4


def exchange(part, width):
    count = lax.axis_size("tile")
    head = part[..., :width, :]
    tail = part[..., -width:, :]
    if count % 2:
        above = lax.ppermute(tail, "tile", [(i, i + 1) for i in range(count - 1)])
        below = lax.ppermute(head, "tile", [(i + 1, i) for i in range(count - 1)])
        return jnp.concatenate([above, part, below], -2)
    odd = lax.axis_index("tile") % 2 == 1
    pairs = lambda first: [(i, i + 1) for i in range(first, count - 1, 2)] + [
        (i + 1, i) for i in range(first, count - 1, 2)
    ]
    far = lax.ppermute(jnp.where(odd, tail, head), "tile", pairs(1))
    near = lax.ppermute(jnp.where(odd, head, tail), "tile", pairs(0))
    above = jnp.where(odd, near, far)
    below = jnp.where(odd, far, near)
    return jnp.concatenate([above, part, below], -2)


def split_exchange(part, width):
    count = lax.axis_size("tile")
    head = part[..., :width, :]
    tail = part[..., -width:, :]
    odd = lax.axis_index("tile") % 2 == 1
    pairs = lambda first: [(i, i + 1) for i in range(first, count - 1, 2)] + [
        (i + 1, i) for i in range(first, count - 1, 2)
    ]
    far = lax.ppermute(jnp.where(odd, tail, head), "tile", pairs(1))
    near = lax.ppermute(jnp.where(odd, head, tail), "tile", pairs(0))
    return near, far, odd


def near_band(part, near, odd):
    zero = jnp.zeros_like(near)
    return jnp.concatenate([jnp.where(odd, near, zero), part, jnp.where(odd, zero, near)], -2)


def full_band(part, near, far, odd):
    return jnp.concatenate([jnp.where(odd, near, far), part, jnp.where(odd, far, near)], -2)


def mem_sum(part):
    count = lax.axis_size("mem")
    if count & (count - 1):
        return lax.psum(part, "mem")

    def partner(stride):
        return lax.ppermute(part, "mem", [(i, i ^ stride) for i in range(count)])

    stride = 1
    while stride < count:
        if stride * 2 < count:
            both = partner(3 * stride)
            near, far = partner(stride), partner(2 * stride)
            part = (part + near) + (far + both)
            stride *= 4
        else:
            part = part + partner(stride)
            stride *= 2
    return part


def diffuse(values, row_coef, col_coef):
    row_flux = row_coef[..., :-1, :] * (values[..., 1:, :] - values[..., :-1, :])
    col_flux = col_coef[..., :, :-1] * (values[..., :, 1:] - values[..., :, :-1])
    zeros_row = jnp.zeros_like(values[..., :1, :])
    zeros_col = jnp.zeros_like(values[..., :, :1])
    values = (
        values
        + jnp.concatenate([row_flux, zeros_row], -2)
        - jnp.concatenate([zeros_row, row_flux], -2)
    )
    return (
        values
        + jnp.concatenate([col_flux, zeros_col], -1)
        - jnp.concatenate([zeros_col, col_flux], -1)
    )


def localize(field, coef_band):
    for repeat in range(STEPS):
        field = diffuse(field, coef_band[0], coef_band[1])
    return field


def per_device(controls, perturbations, jacobian, obs_weight, radar_mask, row_faces, col_faces):
    members, row_count = controls.shape[:2]
    row_index = lax.axis_index("tile") * row_count + lax.broadcasted_iota(
        jnp.int32, row_faces.shape, 0
    )
    row_coef = jnp.where(
        row_index < row_count * lax.axis_size("tile") - 1, row_faces, jnp.zeros_like(row_faces)
    )
    mix = jnp.sum(perturbations.astype(jnp.float32) * jacobian[None], axis=1)
    stacked = jnp.concatenate([controls, row_coef[None], col_faces[None]], 0)
    if lax.axis_size("tile") % 2:
        band = exchange(stacked, STEPS)
        field, coef_band = band[:members], band[members:]
        localized = localize(field, coef_band)[:, STEPS : STEPS + row_count]
        reflect = mem_sum(jnp.sum(mix * localized, 0))
        weighted = radar_mask.astype(jnp.float32) * obs_weight * reflect
        sensitivity = exchange(mix * weighted[None], STEPS)
        return controls + localize(sensitivity, coef_band)[:, STEPS : STEPS + row_count]
    near, far, odd = split_exchange(stacked, STEPS)
    partial = near_band(stacked, near, odd)
    main = localize(partial[:members], partial[members:])[:, STEPS : STEPS + row_count]
    main, far = lax.optimization_barrier((main, far))
    band = full_band(stacked, near, far, odd)
    coef_band = band[members:]
    strip = jnp.where(odd, band[:, row_count - STEPS :], band[:, : 3 * STEPS])
    edge = localize(strip[:members], strip[members:])[:, STEPS : 2 * STEPS]
    localized = jnp.where(
        odd,
        jnp.concatenate([main[:, : row_count - STEPS], edge], 1),
        jnp.concatenate([edge, main[:, STEPS:]], 1),
    )
    reflect = mem_sum(jnp.sum(mix * localized, 0))
    weighted = radar_mask.astype(jnp.float32) * obs_weight * reflect
    near, far, odd = split_exchange(mix * weighted[None], STEPS)
    spread = localize(near_band(mix * weighted[None], near, odd), coef_band)
    spread = spread[:, STEPS : STEPS + row_count]
    spread, far = lax.optimization_barrier((spread, far))
    zero = jnp.zeros_like(far)
    strip = jnp.where(odd, jnp.concatenate([zero, far], 1), jnp.concatenate([far, zero], 1))
    strip_coef = jnp.where(odd, coef_band[:, row_count:], coef_band[:, : 2 * STEPS])
    edge = localize(strip, strip_coef)
    rest = jnp.zeros_like(spread[:, STEPS:])
    edge = jnp.where(
        odd,
        jnp.concatenate([rest, edge[:, :STEPS]], 1),
        jnp.concatenate([edge[:, STEPS:], rest], 1),
    )
    return controls + (spread + edge)


def solution(mesh):
    placed = (
        P("mem", "tile", None),
        P("mem", None, "tile", None),
        P(None, "tile", None),
        P("tile", None),
        P("tile", None),
        P("tile", None),
        P("tile", None),
    )
    return jax.shard_map(
        per_device, mesh=mesh, in_specs=placed, out_specs=P("mem", "tile", None), check_vma=False
    )
```

```python
import jax
import jax.numpy as jnp
from jax import lax
from jax.sharding import PartitionSpec as P

STEPS = 4


def exchange(part, width):
    count = lax.axis_size("tile")
    head = part[..., :width, :]
    tail = part[..., -width:, :]
    if count % 2:
        above = lax.ppermute(tail, "tile", [(i, i + 1) for i in range(count - 1)])
        below = lax.ppermute(head, "tile", [(i + 1, i) for i in range(count - 1)])
        return jnp.concatenate([above, part, below], -2)
    odd = lax.axis_index("tile") % 2 == 1
    pairs = lambda first: [(i, i + 1) for i in range(first, count - 1, 2)] + [
        (i + 1, i) for i in range(first, count - 1, 2)
    ]
    far = lax.ppermute(jnp.where(odd, tail, head), "tile", pairs(1))
    near = lax.ppermute(jnp.where(odd, head, tail), "tile", pairs(0))
    above = jnp.where(odd, near, far)
    below = jnp.where(odd, far, near)
    return jnp.concatenate([above, part, below], -2)


def split_exchange(part, width):
    count = lax.axis_size("tile")
    head = part[..., :width, :]
    tail = part[..., -width:, :]
    odd = lax.axis_index("tile") % 2 == 1
    pairs = lambda first: [(i, i + 1) for i in range(first, count - 1, 2)] + [
        (i + 1, i) for i in range(first, count - 1, 2)
    ]
    far = lax.ppermute(jnp.where(odd, tail, head), "tile", pairs(1))
    near = lax.ppermute(jnp.where(odd, head, tail), "tile", pairs(0))
    return near, far, odd


def near_band(part, near, odd):
    zero = jnp.zeros_like(near)
    return jnp.concatenate([jnp.where(odd, near, zero), part, jnp.where(odd, zero, near)], -2)


def full_band(part, near, far, odd):
    return jnp.concatenate([jnp.where(odd, near, far), part, jnp.where(odd, far, near)], -2)


def mem_sum(part):
    count = lax.axis_size("mem")
    if count & (count - 1):
        return lax.psum(part, "mem")

    def partner(stride):
        return lax.ppermute(part, "mem", [(i, i ^ stride) for i in range(count)])

    stride = 1
    while stride < count:
        if stride * 2 < count:
            near, far, both = partner(stride), partner(2 * stride), partner(3 * stride)
            part = (part + near) + (far + both)
            stride *= 4
        else:
            part = part + partner(stride)
            stride *= 2
    return part


def diffuse(values, row_coef, col_coef):
    row_flux = row_coef[..., :-1, :] * (values[..., 1:, :] - values[..., :-1, :])
    col_flux = col_coef[..., :, :-1] * (values[..., :, 1:] - values[..., :, :-1])
    zeros_row = jnp.zeros_like(values[..., :1, :])
    zeros_col = jnp.zeros_like(values[..., :, :1])
    values = (
        values
        + jnp.concatenate([row_flux, zeros_row], -2)
        - jnp.concatenate([zeros_row, row_flux], -2)
    )
    return (
        values
        + jnp.concatenate([col_flux, zeros_col], -1)
        - jnp.concatenate([zeros_col, col_flux], -1)
    )


def localize(field, coef_band):
    for repeat in range(STEPS):
        field = diffuse(field, coef_band[0], coef_band[1])
    return field


def per_device(controls, perturbations, jacobian, obs_weight, radar_mask, row_faces, col_faces):
    members, row_count = controls.shape[:2]
    row_index = lax.axis_index("tile") * row_count + lax.broadcasted_iota(
        jnp.int32, row_faces.shape, 0
    )
    row_coef = jnp.where(
        row_index < row_count * lax.axis_size("tile") - 1, row_faces, jnp.zeros_like(row_faces)
    )
    mix = jnp.sum(perturbations.astype(jnp.float32) * jacobian[None], axis=1)
    stacked = jnp.concatenate([controls, row_coef[None], col_faces[None]], 0)
    if lax.axis_size("tile") % 2:
        band = exchange(stacked, STEPS)
        field, coef_band = band[:members], band[members:]
        localized = localize(field, coef_band)[:, STEPS : STEPS + row_count]
        reflect = mem_sum(jnp.sum(mix * localized, 0))
        weighted = radar_mask.astype(jnp.float32) * obs_weight * reflect
        sensitivity = exchange(mix * weighted[None], STEPS)
        return controls + localize(sensitivity, coef_band)[:, STEPS : STEPS + row_count]
    near, far, odd = split_exchange(stacked, STEPS)
    partial = near_band(stacked, near, odd)
    main = localize(partial[:members], partial[members:])[:, STEPS : STEPS + row_count]
    main, far = lax.optimization_barrier((main, far))
    band = full_band(stacked, near, far, odd)
    coef_band = band[members:]
    strip = jnp.where(odd, band[:, row_count - STEPS :], band[:, : 3 * STEPS])
    edge = localize(strip[:members], strip[members:])[:, STEPS : 2 * STEPS]
    localized = jnp.where(
        odd,
        jnp.concatenate([main[:, : row_count - STEPS], edge], 1),
        jnp.concatenate([edge, main[:, STEPS:]], 1),
    )
    reflect = mem_sum(jnp.sum(mix * localized, 0))
    weighted = radar_mask.astype(jnp.float32) * obs_weight * reflect
    near, far, odd = split_exchange(mix * weighted[None], STEPS)
    spread = localize(near_band(mix * weighted[None], near, odd), coef_band)
    base = controls + spread[:, STEPS : STEPS + row_count]
    base, far = lax.optimization_barrier((base, far))
    zero = jnp.zeros_like(far)
    strip = jnp.where(odd, jnp.concatenate([zero, far], 1), jnp.concatenate([far, zero], 1))
    strip_coef = jnp.where(odd, coef_band[:, row_count:], coef_band[:, : 2 * STEPS])
    edge = localize(strip, strip_coef)
    edge = jnp.where(odd, edge[:, :STEPS], edge[:, STEPS:])
    first = jnp.where(odd, row_count - STEPS, 0)
    current = lax.dynamic_slice_in_dim(base, first, STEPS, axis=1)
    return lax.dynamic_update_slice_in_dim(base, current + edge, first, axis=1)


def solution(mesh):
    placed = (
        P("mem", "tile", None),
        P("mem", None, "tile", None),
        P(None, "tile", None),
        P("tile", None),
        P("tile", None),
        P("tile", None),
        P("tile", None),
    )
    return jax.shard_map(
        per_device, mesh=mesh, in_specs=placed, out_specs=P("mem", "tile", None), check_vma=False
    )
```

```python
import jax
import jax.numpy as jnp
from jax import lax
from jax.sharding import PartitionSpec as P

STEPS = 4


def exchange(part, width):
    count = lax.axis_size("tile")
    head = part[..., :width, :]
    tail = part[..., -width:, :]
    if count % 2:
        above = lax.ppermute(tail, "tile", [(i, i + 1) for i in range(count - 1)])
        below = lax.ppermute(head, "tile", [(i + 1, i) for i in range(count - 1)])
        return jnp.concatenate([above, part, below], -2)
    odd = lax.axis_index("tile") % 2 == 1
    pairs = lambda first: [(i, i + 1) for i in range(first, count - 1, 2)] + [
        (i + 1, i) for i in range(first, count - 1, 2)
    ]
    far = lax.ppermute(jnp.where(odd, tail, head), "tile", pairs(1))
    near = lax.ppermute(jnp.where(odd, head, tail), "tile", pairs(0))
    above = jnp.where(odd, near, far)
    below = jnp.where(odd, far, near)
    return jnp.concatenate([above, part, below], -2)


def split_exchange(part, width):
    count = lax.axis_size("tile")
    head = part[..., :width, :]
    tail = part[..., -width:, :]
    odd = lax.axis_index("tile") % 2 == 1
    pairs = lambda first: [(i, i + 1) for i in range(first, count - 1, 2)] + [
        (i + 1, i) for i in range(first, count - 1, 2)
    ]
    far = lax.ppermute(jnp.where(odd, tail, head), "tile", pairs(1))
    near = lax.ppermute(jnp.where(odd, head, tail), "tile", pairs(0))
    return near, far, odd


def near_band(part, near, odd):
    zero = jnp.zeros_like(near)
    return jnp.concatenate([jnp.where(odd, near, zero), part, jnp.where(odd, zero, near)], -2)


def full_band(part, near, far, odd):
    return jnp.concatenate([jnp.where(odd, near, far), part, jnp.where(odd, far, near)], -2)


def mem_sum(part):
    count = lax.axis_size("mem")
    if count & (count - 1):
        return lax.psum(part, "mem")

    def partner(stride):
        return lax.ppermute(part, "mem", [(i, i ^ stride) for i in range(count)])

    stride = 1
    while stride < count:
        if stride * 2 < count:
            near, far, both = partner(stride), partner(2 * stride), partner(3 * stride)
            part = (part + near) + (far + both)
            stride *= 4
        else:
            part = part + partner(stride)
            stride *= 2
    return part


def diffuse(values, row_coef, col_coef):
    row_flux = row_coef[..., :-1, :] * (values[..., 1:, :] - values[..., :-1, :])
    col_flux = col_coef[..., :, :-1] * (values[..., :, 1:] - values[..., :, :-1])
    zeros_row = jnp.zeros_like(values[..., :1, :])
    zeros_col = jnp.zeros_like(values[..., :, :1])
    values = (
        values
        + jnp.concatenate([row_flux, zeros_row], -2)
        - jnp.concatenate([zeros_row, row_flux], -2)
    )
    return (
        values
        + jnp.concatenate([col_flux, zeros_col], -1)
        - jnp.concatenate([zeros_col, col_flux], -1)
    )


def localize(field, coef_band):
    for repeat in range(STEPS):
        field = diffuse(field, coef_band[0], coef_band[1])
    return field


def localize_inner(field, coef_band):
    for repeat in range(STEPS):
        field = diffuse(field, coef_band[0], coef_band[1])[..., 1:-1, :]
        coef_band = coef_band[..., 1:-1, :]
    return field


def per_device(controls, perturbations, jacobian, obs_weight, radar_mask, row_faces, col_faces):
    members, row_count = controls.shape[:2]
    row_index = lax.axis_index("tile") * row_count + lax.broadcasted_iota(
        jnp.int32, row_faces.shape, 0
    )
    row_coef = jnp.where(
        row_index < row_count * lax.axis_size("tile") - 1, row_faces, jnp.zeros_like(row_faces)
    )
    mix = jnp.sum(perturbations.astype(jnp.float32) * jacobian[None], axis=1)
    stacked = jnp.concatenate([controls, row_coef[None], col_faces[None]], 0)
    if lax.axis_size("tile") % 2:
        band = exchange(stacked, STEPS)
        field, coef_band = band[:members], band[members:]
        localized = localize(field, coef_band)[:, STEPS : STEPS + row_count]
        reflect = mem_sum(jnp.sum(mix * localized, 0))
        weighted = radar_mask.astype(jnp.float32) * obs_weight * reflect
        sensitivity = exchange(mix * weighted[None], STEPS)
        return controls + localize(sensitivity, coef_band)[:, STEPS : STEPS + row_count]
    near, far, odd = split_exchange(stacked, STEPS)
    partial = near_band(stacked, near, odd)
    main = localize(partial[:members], partial[members:])[:, STEPS : STEPS + row_count]
    main, far = lax.optimization_barrier((main, far))
    band = full_band(stacked, near, far, odd)
    coef_band = band[members:]
    strip = jnp.where(odd, band[:, row_count - STEPS :], band[:, : 3 * STEPS])
    edge = localize_inner(strip[:members], strip[members:])
    localized = jnp.where(
        odd,
        jnp.concatenate([main[:, : row_count - STEPS], edge], 1),
        jnp.concatenate([edge, main[:, STEPS:]], 1),
    )
    reflect = mem_sum(jnp.sum(mix * localized, 0))
    weighted = radar_mask.astype(jnp.float32) * obs_weight * reflect
    near, far, odd = split_exchange(mix * weighted[None], STEPS)
    spread = localize(near_band(mix * weighted[None], near, odd), coef_band)
    spread = spread[:, STEPS : STEPS + row_count]
    spread, far = lax.optimization_barrier((spread, far))
    zero = jnp.zeros_like(far)
    strip = jnp.where(odd, jnp.concatenate([zero, far], 1), jnp.concatenate([far, zero], 1))
    strip_coef = jnp.where(odd, coef_band[:, row_count:], coef_band[:, : 2 * STEPS])
    edge = localize(strip, strip_coef)
    rest = jnp.zeros_like(spread[:, STEPS:])
    edge = jnp.where(
        odd,
        jnp.concatenate([rest, edge[:, :STEPS]], 1),
        jnp.concatenate([edge[:, STEPS:], rest], 1),
    )
    return controls + (spread + edge)


def solution(mesh):
    placed = (
        P("mem", "tile", None),
        P("mem", None, "tile", None),
        P(None, "tile", None),
        P("tile", None),
        P("tile", None),
        P("tile", None),
        P("tile", None),
    )
    return jax.shard_map(
        per_device, mesh=mesh, in_specs=placed, out_specs=P("mem", "tile", None), check_vma=False
    )
```

```python
import jax
import jax.numpy as jnp
from jax import lax
from jax.sharding import PartitionSpec as P

STEPS = 4


def exchange(part, width):
    count = lax.axis_size("tile")
    head = part[..., :width, :]
    tail = part[..., -width:, :]
    if count % 2:
        above = lax.ppermute(tail, "tile", [(i, i + 1) for i in range(count - 1)])
        below = lax.ppermute(head, "tile", [(i + 1, i) for i in range(count - 1)])
        return jnp.concatenate([above, part, below], -2)
    odd = lax.axis_index("tile") % 2 == 1
    pairs = lambda first: [(i, i + 1) for i in range(first, count - 1, 2)] + [
        (i + 1, i) for i in range(first, count - 1, 2)
    ]
    far = lax.ppermute(jnp.where(odd, tail, head), "tile", pairs(1))
    near = lax.ppermute(jnp.where(odd, head, tail), "tile", pairs(0))
    above = jnp.where(odd, near, far)
    below = jnp.where(odd, far, near)
    return jnp.concatenate([above, part, below], -2)


def split_exchange(part, width):
    count = lax.axis_size("tile")
    head = part[..., :width, :]
    tail = part[..., -width:, :]
    odd = lax.axis_index("tile") % 2 == 1
    pairs = lambda first: [(i, i + 1) for i in range(first, count - 1, 2)] + [
        (i + 1, i) for i in range(first, count - 1, 2)
    ]
    far = lax.ppermute(jnp.where(odd, tail, head), "tile", pairs(1))
    near = lax.ppermute(jnp.where(odd, head, tail), "tile", pairs(0))
    return near, far, odd


def near_band(part, near, odd):
    zero = jnp.zeros_like(near)
    return jnp.concatenate([jnp.where(odd, near, zero), part, jnp.where(odd, zero, near)], -2)


def full_band(part, near, far, odd):
    return jnp.concatenate([jnp.where(odd, near, far), part, jnp.where(odd, far, near)], -2)


def mem_sum(part):
    count = lax.axis_size("mem")
    if count & (count - 1):
        return lax.psum(part, "mem")

    def partner(stride):
        return lax.ppermute(part, "mem", [(i, i ^ stride) for i in range(count)])

    stride = 1
    while stride < count:
        if stride * 2 < count:
            near, far, both = partner(stride), partner(2 * stride), partner(3 * stride)
            part = (part + near) + (far + both)
            stride *= 4
        else:
            part = part + partner(stride)
            stride *= 2
    return part


def diffuse(values, row_coef, col_coef):
    row_flux = row_coef[..., :-1, :] * (values[..., 1:, :] - values[..., :-1, :])
    col_flux = col_coef[..., :, :-1] * (values[..., :, 1:] - values[..., :, :-1])
    zeros_row = jnp.zeros_like(values[..., :1, :])
    zeros_col = jnp.zeros_like(values[..., :, :1])
    values = (
        values
        + jnp.concatenate([row_flux, zeros_row], -2)
        - jnp.concatenate([zeros_row, row_flux], -2)
    )
    return (
        values
        + jnp.concatenate([col_flux, zeros_col], -1)
        - jnp.concatenate([zeros_col, col_flux], -1)
    )


def localize(field, coef_band):
    for repeat in range(STEPS):
        field = diffuse(field, coef_band[0], coef_band[1])
    return field


def localize_inner(field, coef_band):
    for repeat in range(STEPS):
        field = diffuse(field, coef_band[0], coef_band[1])[..., 1:-1, :]
        coef_band = coef_band[..., 1:-1, :]
    return field


def per_device(controls, perturbations, jacobian, obs_weight, radar_mask, row_faces, col_faces):
    members, row_count = controls.shape[:2]
    row_index = lax.axis_index("tile") * row_count + lax.broadcasted_iota(
        jnp.int32, row_faces.shape, 0
    )
    row_coef = jnp.where(
        row_index < row_count * lax.axis_size("tile") - 1, row_faces, jnp.zeros_like(row_faces)
    )
    mix = jnp.sum(perturbations.astype(jnp.float32) * jacobian[None], axis=1)
    stacked = jnp.concatenate([controls, row_coef[None], col_faces[None]], 0)
    if lax.axis_size("tile") % 2:
        band = exchange(stacked, STEPS)
        field, coef_band = band[:members], band[members:]
        localized = localize(field, coef_band)[:, STEPS : STEPS + row_count]
        reflect = mem_sum(jnp.sum(mix * localized, 0))
        weighted = radar_mask.astype(jnp.float32) * obs_weight * reflect
        sensitivity = exchange(mix * weighted[None], STEPS)
        return controls + localize(sensitivity, coef_band)[:, STEPS : STEPS + row_count]
    near, far, odd = split_exchange(stacked, STEPS)
    partial = near_band(stacked, near, odd)
    main = localize_inner(partial[:members], partial[members:])
    main, far = lax.optimization_barrier((main, far))
    band = full_band(stacked, near, far, odd)
    coef_band = band[members:]
    strip = jnp.where(odd, band[:, row_count - STEPS :], band[:, : 3 * STEPS])
    edge = localize_inner(strip[:members], strip[members:])
    localized = jnp.where(
        odd,
        jnp.concatenate([main[:, : row_count - STEPS], edge], 1),
        jnp.concatenate([edge, main[:, STEPS:]], 1),
    )
    reflect = mem_sum(jnp.sum(mix * localized, 0))
    weighted = radar_mask.astype(jnp.float32) * obs_weight * reflect
    near, far, odd = split_exchange(mix * weighted[None], STEPS)
    spread = localize_inner(near_band(mix * weighted[None], near, odd), coef_band)
    spread, far = lax.optimization_barrier((spread, far))
    zero = jnp.zeros_like(far)
    strip = jnp.where(odd, jnp.concatenate([zero, far], 1), jnp.concatenate([far, zero], 1))
    strip_coef = jnp.where(odd, coef_band[:, row_count:], coef_band[:, : 2 * STEPS])
    edge = localize(strip, strip_coef)
    rest = jnp.zeros_like(spread[:, STEPS:])
    edge = jnp.where(
        odd,
        jnp.concatenate([rest, edge[:, :STEPS]], 1),
        jnp.concatenate([edge[:, STEPS:], rest], 1),
    )
    return controls + (spread + edge)


def solution(mesh):
    placed = (
        P("mem", "tile", None),
        P("mem", None, "tile", None),
        P(None, "tile", None),
        P("tile", None),
        P("tile", None),
        P("tile", None),
        P("tile", None),
    )
    return jax.shard_map(
        per_device, mesh=mesh, in_specs=placed, out_specs=P("mem", "tile", None), check_vma=False
    )
```

```python
import jax
import jax.numpy as jnp
from jax import lax
from jax.sharding import PartitionSpec as P

STEPS = 4


def exchange(part, width):
    count = lax.axis_size("tile")
    head = part[..., :width, :]
    tail = part[..., -width:, :]
    if count % 2:
        above = lax.ppermute(tail, "tile", [(i, i + 1) for i in range(count - 1)])
        below = lax.ppermute(head, "tile", [(i + 1, i) for i in range(count - 1)])
        return jnp.concatenate([above, part, below], -2)
    odd = lax.axis_index("tile") % 2 == 1
    pairs = lambda first: [(i, i + 1) for i in range(first, count - 1, 2)] + [
        (i + 1, i) for i in range(first, count - 1, 2)
    ]
    far = lax.ppermute(jnp.where(odd, tail, head), "tile", pairs(1))
    near = lax.ppermute(jnp.where(odd, head, tail), "tile", pairs(0))
    above = jnp.where(odd, near, far)
    below = jnp.where(odd, far, near)
    return jnp.concatenate([above, part, below], -2)


def split_exchange(part, width):
    count = lax.axis_size("tile")
    head = part[..., :width, :]
    tail = part[..., -width:, :]
    odd = lax.axis_index("tile") % 2 == 1
    pairs = lambda first: [(i, i + 1) for i in range(first, count - 1, 2)] + [
        (i + 1, i) for i in range(first, count - 1, 2)
    ]
    far = lax.ppermute(jnp.where(odd, tail, head), "tile", pairs(1))
    near = lax.ppermute(jnp.where(odd, head, tail), "tile", pairs(0))
    return near, far, odd


def near_band(part, near, odd):
    zero = jnp.zeros_like(near)
    return jnp.concatenate([jnp.where(odd, near, zero), part, jnp.where(odd, zero, near)], -2)


def full_band(part, near, far, odd):
    return jnp.concatenate([jnp.where(odd, near, far), part, jnp.where(odd, far, near)], -2)


def mem_sum(part):
    count = lax.axis_size("mem")
    if count & (count - 1):
        return lax.psum(part, "mem")

    def partner(stride):
        return lax.ppermute(part, "mem", [(i, i ^ stride) for i in range(count)])

    stride = 1
    while stride < count:
        if stride * 2 < count:
            near, far, both = partner(stride), partner(2 * stride), partner(3 * stride)
            part = (part + near) + (far + both)
            stride *= 4
        else:
            part = part + partner(stride)
            stride *= 2
    return part


def diffuse(values, row_coef, col_coef):
    row_flux = row_coef[..., :-1, :] * (values[..., 1:, :] - values[..., :-1, :])
    col_flux = col_coef[..., :, :-1] * (values[..., :, 1:] - values[..., :, :-1])
    zeros_row = jnp.zeros_like(values[..., :1, :])
    zeros_col = jnp.zeros_like(values[..., :, :1])
    values = (
        values
        + jnp.concatenate([row_flux, zeros_row], -2)
        - jnp.concatenate([zeros_row, row_flux], -2)
    )
    return (
        values
        + jnp.concatenate([col_flux, zeros_col], -1)
        - jnp.concatenate([zeros_col, col_flux], -1)
    )


def localize(field, coef_band):
    for repeat in range(STEPS):
        field = diffuse(field, coef_band[0], coef_band[1])
    return field


def localize_inner(field, coef_band):
    for repeat in range(STEPS):
        field = diffuse(field, coef_band[0], coef_band[1])[..., 1:-1, :]
        coef_band = coef_band[..., 1:-1, :]
    return field


def per_device(controls, perturbations, jacobian, obs_weight, radar_mask, row_faces, col_faces):
    members, row_count = controls.shape[:2]
    row_index = lax.axis_index("tile") * row_count + lax.broadcasted_iota(
        jnp.int32, row_faces.shape, 0
    )
    row_coef = jnp.where(
        row_index < row_count * lax.axis_size("tile") - 1, row_faces, jnp.zeros_like(row_faces)
    )
    mix = jnp.sum(perturbations.astype(jnp.float32) * jacobian[None], axis=1)
    stacked = jnp.concatenate([controls, row_coef[None], col_faces[None]], 0)
    if lax.axis_size("tile") % 2:
        band = exchange(stacked, STEPS)
        field, coef_band = band[:members], band[members:]
        localized = localize(field, coef_band)[:, STEPS : STEPS + row_count]
        reflect = mem_sum(jnp.sum(mix * localized, 0))
        weighted = radar_mask.astype(jnp.float32) * obs_weight * reflect
        sensitivity = exchange(mix * weighted[None], STEPS)
        return controls + localize(sensitivity, coef_band)[:, STEPS : STEPS + row_count]
    near, far, odd = split_exchange(stacked, STEPS)
    partial = near_band(stacked, near, odd)
    main = localize_inner(partial[:members], partial[members:])
    main, far = lax.optimization_barrier((main, far))
    band = full_band(stacked, near, far, odd)
    coef_band = band[members:]
    strip = jnp.where(odd, band[:, row_count - STEPS :], band[:, : 3 * STEPS])
    edge = localize_inner(strip[:members], strip[members:])
    localized = jnp.where(
        odd,
        jnp.concatenate([main[:, : row_count - STEPS], edge], 1),
        jnp.concatenate([edge, main[:, STEPS:]], 1),
    )
    reflect = mem_sum(jnp.sum(mix * localized, 0))
    weighted = radar_mask.astype(jnp.float32) * obs_weight * reflect
    near, far, odd = split_exchange(mix * weighted[None], STEPS)
    spread = localize(near_band(mix * weighted[None], near, odd), coef_band)
    spread = spread[:, STEPS : STEPS + row_count]
    spread, far = lax.optimization_barrier((spread, far))
    zero = jnp.zeros_like(far)
    strip = jnp.where(odd, jnp.concatenate([zero, far], 1), jnp.concatenate([far, zero], 1))
    strip_coef = jnp.where(odd, coef_band[:, row_count:], coef_band[:, : 2 * STEPS])
    edge = localize(strip, strip_coef)
    rest = jnp.zeros_like(spread[:, STEPS:])
    edge = jnp.where(
        odd,
        jnp.concatenate([rest, edge[:, :STEPS]], 1),
        jnp.concatenate([edge[:, STEPS:], rest], 1),
    )
    return controls + (spread + edge)


def solution(mesh):
    placed = (
        P("mem", "tile", None),
        P("mem", None, "tile", None),
        P(None, "tile", None),
        P("tile", None),
        P("tile", None),
        P("tile", None),
        P("tile", None),
    )
    return jax.shard_map(
        per_device, mesh=mesh, in_specs=placed, out_specs=P("mem", "tile", None), check_vma=False
    )
```

```python
import jax
import jax.numpy as jnp
from jax import lax
from jax.sharding import PartitionSpec as P

STEPS = 4


def exchange(part, width):
    count = lax.axis_size("tile")
    head = part[..., :width, :]
    tail = part[..., -width:, :]
    if count % 2:
        above = lax.ppermute(tail, "tile", [(i, i + 1) for i in range(count - 1)])
        below = lax.ppermute(head, "tile", [(i + 1, i) for i in range(count - 1)])
        return jnp.concatenate([above, part, below], -2)
    odd = lax.axis_index("tile") % 2 == 1
    pairs = lambda first: [(i, i + 1) for i in range(first, count - 1, 2)] + [
        (i + 1, i) for i in range(first, count - 1, 2)
    ]
    far = lax.ppermute(jnp.where(odd, tail, head), "tile", pairs(1))
    near = lax.ppermute(jnp.where(odd, head, tail), "tile", pairs(0))
    above = jnp.where(odd, near, far)
    below = jnp.where(odd, far, near)
    return jnp.concatenate([above, part, below], -2)


def split_exchange(part, width):
    count = lax.axis_size("tile")
    head = part[..., :width, :]
    tail = part[..., -width:, :]
    odd = lax.axis_index("tile") % 2 == 1
    pairs = lambda first: [(i, i + 1) for i in range(first, count - 1, 2)] + [
        (i + 1, i) for i in range(first, count - 1, 2)
    ]
    far = lax.ppermute(jnp.where(odd, tail, head), "tile", pairs(1))
    near = lax.ppermute(jnp.where(odd, head, tail), "tile", pairs(0))
    return near, far, odd


def near_band(part, near, odd):
    zero = jnp.zeros_like(near)
    return jnp.concatenate([jnp.where(odd, near, zero), part, jnp.where(odd, zero, near)], -2)


def full_band(part, near, far, odd):
    return jnp.concatenate([jnp.where(odd, near, far), part, jnp.where(odd, far, near)], -2)


def mem_sum(part):
    count = lax.axis_size("mem")
    if count & (count - 1):
        return lax.psum(part, "mem")

    def partner(stride):
        return lax.ppermute(part, "mem", [(i, i ^ stride) for i in range(count)])

    stride = 1
    while stride < count:
        if stride * 2 < count:
            near, far, both = partner(stride), partner(2 * stride), partner(3 * stride)
            part = (part + near) + (far + both)
            stride *= 4
        else:
            part = part + partner(stride)
            stride *= 2
    return part


def diffuse(values, row_coef, col_coef):
    row_flux = row_coef[..., :-1, :] * (values[..., 1:, :] - values[..., :-1, :])
    col_flux = col_coef[..., :, :-1] * (values[..., :, 1:] - values[..., :, :-1])
    zeros_row = jnp.zeros_like(values[..., :1, :])
    zeros_col = jnp.zeros_like(values[..., :, :1])
    values = (
        values
        + jnp.concatenate([row_flux, zeros_row], -2)
        - jnp.concatenate([zeros_row, row_flux], -2)
    )
    return (
        values
        + jnp.concatenate([col_flux, zeros_col], -1)
        - jnp.concatenate([zeros_col, col_flux], -1)
    )


def localize(field, coef_band):
    for repeat in range(STEPS):
        field = diffuse(field, coef_band[0], coef_band[1])
    return field


def localize_inner(field, coef_band):
    for repeat in range(STEPS):
        field = diffuse(field, coef_band[0], coef_band[1])[..., 1:-1, :]
        coef_band = coef_band[..., 1:-1, :]
    return field


def per_device(controls, perturbations, jacobian, obs_weight, radar_mask, row_faces, col_faces):
    members, row_count = controls.shape[:2]
    last_row = row_count * lax.axis_size("tile") - 1 - lax.axis_index("tile") * row_count

    def masked(coefs):
        band_row = lax.broadcasted_iota(jnp.int32, coefs.shape, 1) - STEPS
        keep = (band_row != last_row) | (lax.broadcasted_iota(jnp.int32, coefs.shape, 0) > 0)
        return jnp.where(keep, coefs, jnp.zeros_like(coefs))

    row_coef = row_faces
    mix = jnp.sum(perturbations.astype(jnp.float32) * jacobian[None], axis=1)
    stacked = jnp.concatenate([controls, row_coef[None], col_faces[None]], 0)
    if lax.axis_size("tile") % 2:
        band = exchange(stacked, STEPS)
        field, coef_band = band[:members], masked(band[members:])
        localized = localize(field, coef_band)[:, STEPS : STEPS + row_count]
        reflect = mem_sum(jnp.sum(mix * localized, 0))
        weighted = radar_mask.astype(jnp.float32) * obs_weight * reflect
        sensitivity = exchange(mix * weighted[None], STEPS)
        return controls + localize(sensitivity, coef_band)[:, STEPS : STEPS + row_count]
    near, far, odd = split_exchange(stacked, STEPS)
    partial = near_band(stacked, near, odd)
    main = localize(partial[:members], masked(partial[members:]))[:, STEPS : STEPS + row_count]
    main, far = lax.optimization_barrier((main, far))
    band = full_band(stacked, near, far, odd)
    band = jnp.concatenate([band[:members], masked(band[members:])], 0)
    coef_band = band[members:]
    strip = jnp.where(odd, band[:, row_count - STEPS :], band[:, : 3 * STEPS])
    edge = localize_inner(strip[:members], strip[members:])
    localized = jnp.where(
        odd,
        jnp.concatenate([main[:, : row_count - STEPS], edge], 1),
        jnp.concatenate([edge, main[:, STEPS:]], 1),
    )
    reflect = mem_sum(jnp.sum(mix * localized, 0))
    weighted = radar_mask.astype(jnp.float32) * obs_weight * reflect
    near, far, odd = split_exchange(mix * weighted[None], STEPS)
    spread = localize(near_band(mix * weighted[None], near, odd), coef_band)
    spread = spread[:, STEPS : STEPS + row_count]
    spread, far = lax.optimization_barrier((spread, far))
    zero = jnp.zeros_like(far)
    strip = jnp.where(odd, jnp.concatenate([zero, far], 1), jnp.concatenate([far, zero], 1))
    strip_coef = jnp.where(odd, coef_band[:, row_count:], coef_band[:, : 2 * STEPS])
    edge = localize(strip, strip_coef)
    rest = jnp.zeros_like(spread[:, STEPS:])
    edge = jnp.where(
        odd,
        jnp.concatenate([rest, edge[:, :STEPS]], 1),
        jnp.concatenate([edge[:, STEPS:], rest], 1),
    )
    return controls + (spread + edge)


def solution(mesh):
    placed = (
        P("mem", "tile", None),
        P("mem", None, "tile", None),
        P(None, "tile", None),
        P("tile", None),
        P("tile", None),
        P("tile", None),
        P("tile", None),
    )
    return jax.shard_map(
        per_device, mesh=mesh, in_specs=placed, out_specs=P("mem", "tile", None), check_vma=False
    )
```

```python
import jax
import jax.numpy as jnp
from jax import lax
from jax.sharding import PartitionSpec as P

STEPS = 4


def exchange(part, width):
    count = lax.axis_size("tile")
    head = part[..., :width, :]
    tail = part[..., -width:, :]
    if count % 2:
        above = lax.ppermute(tail, "tile", [(i, i + 1) for i in range(count - 1)])
        below = lax.ppermute(head, "tile", [(i + 1, i) for i in range(count - 1)])
        return jnp.concatenate([above, part, below], -2)
    odd = lax.axis_index("tile") % 2 == 1
    pairs = lambda first: [(i, i + 1) for i in range(first, count - 1, 2)] + [
        (i + 1, i) for i in range(first, count - 1, 2)
    ]
    far = lax.ppermute(jnp.where(odd, tail, head), "tile", pairs(1))
    near = lax.ppermute(jnp.where(odd, head, tail), "tile", pairs(0))
    above = jnp.where(odd, near, far)
    below = jnp.where(odd, far, near)
    return jnp.concatenate([above, part, below], -2)


def split_exchange(part, width):
    count = lax.axis_size("tile")
    head = part[..., :width, :]
    tail = part[..., -width:, :]
    odd = lax.axis_index("tile") % 2 == 1
    pairs = lambda first: [(i, i + 1) for i in range(first, count - 1, 2)] + [
        (i + 1, i) for i in range(first, count - 1, 2)
    ]
    far = lax.ppermute(jnp.where(odd, tail, head), "tile", pairs(1))
    near = lax.ppermute(jnp.where(odd, head, tail), "tile", pairs(0))
    return near, far, odd


def near_band(part, near, odd):
    zero = jnp.zeros_like(near)
    return jnp.concatenate([jnp.where(odd, near, zero), part, jnp.where(odd, zero, near)], -2)


def full_band(part, near, far, odd):
    return jnp.concatenate([jnp.where(odd, near, far), part, jnp.where(odd, far, near)], -2)


def mem_sum(part):
    count = lax.axis_size("mem")
    if count & (count - 1):
        return lax.psum(part, "mem")

    def partner(stride):
        return lax.ppermute(part, "mem", [(i, i ^ stride) for i in range(count)])

    stride = 1
    while stride < count:
        if stride * 2 < count:
            near, far, both = partner(stride), partner(2 * stride), partner(3 * stride)
            part = (part + near) + (far + both)
            stride *= 4
        else:
            part = part + partner(stride)
            stride *= 2
    return part


def diffuse(values, row_coef, col_coef):
    row_flux = row_coef[..., :-1, :] * (values[..., 1:, :] - values[..., :-1, :])
    col_flux = col_coef[..., :, :-1] * (values[..., :, 1:] - values[..., :, :-1])
    zeros_row = jnp.zeros_like(values[..., :1, :])
    zeros_col = jnp.zeros_like(values[..., :, :1])
    values = (
        values
        + jnp.concatenate([row_flux, zeros_row], -2)
        - jnp.concatenate([zeros_row, row_flux], -2)
    )
    return (
        values
        + jnp.concatenate([col_flux, zeros_col], -1)
        - jnp.concatenate([zeros_col, col_flux], -1)
    )


def localize(field, coef_band):
    for repeat in range(STEPS):
        field = diffuse(field, coef_band[0], coef_band[1])
    return field


def localize_inner(field, coef_band):
    for repeat in range(STEPS):
        field = diffuse(field, coef_band[0], coef_band[1])[..., 1:-1, :]
        coef_band = coef_band[..., 1:-1, :]
    return field


def per_device(controls, perturbations, jacobian, obs_weight, radar_mask, row_faces, col_faces):
    members, row_count = controls.shape[:2]
    row_index = lax.axis_index("tile") * row_count + lax.broadcasted_iota(
        jnp.int32, row_faces.shape, 0
    )
    row_coef = jnp.where(
        row_index < row_count * lax.axis_size("tile") - 1, row_faces, jnp.zeros_like(row_faces)
    )
    mix = jnp.sum(perturbations.astype(jnp.float32) * jacobian[None], axis=1)
    stacked = jnp.concatenate([controls, row_coef[None], col_faces[None]], 0)
    if lax.axis_size("tile") % 2:
        band = exchange(stacked, STEPS)
        field, coef_band = band[:members], band[members:]
        localized = localize(field, coef_band)[:, STEPS : STEPS + row_count]
        reflect = mem_sum(jnp.sum(mix * localized, 0))
        weighted = radar_mask.astype(jnp.float32) * obs_weight * reflect
        sensitivity = exchange(mix * weighted[None], STEPS)
        return controls + localize(sensitivity, coef_band)[:, STEPS : STEPS + row_count]
    near, far, odd = split_exchange(stacked, STEPS)
    partial = near_band(stacked, near, odd)
    main = localize(partial[:members], partial[members:])[:, STEPS : STEPS + row_count]
    main, far = lax.optimization_barrier((main, far))
    band = full_band(stacked, near, far, odd)
    coef_band = band[members:]
    strip = lax.dynamic_slice_in_dim(
        band, jnp.where(odd, row_count - STEPS, 0), 3 * STEPS, axis=1
    )
    edge = localize_inner(strip[:members], strip[members:])
    localized = jnp.where(
        odd,
        jnp.concatenate([main[:, : row_count - STEPS], edge], 1),
        jnp.concatenate([edge, main[:, STEPS:]], 1),
    )
    reflect = mem_sum(jnp.sum(mix * localized, 0))
    weighted = radar_mask.astype(jnp.float32) * obs_weight * reflect
    near, far, odd = split_exchange(mix * weighted[None], STEPS)
    spread = localize(near_band(mix * weighted[None], near, odd), coef_band)
    spread = spread[:, STEPS : STEPS + row_count]
    spread, far = lax.optimization_barrier((spread, far))
    zero = jnp.zeros_like(far)
    strip = jnp.where(odd, jnp.concatenate([zero, far], 1), jnp.concatenate([far, zero], 1))
    strip_coef = jnp.where(odd, coef_band[:, row_count:], coef_band[:, : 2 * STEPS])
    edge = localize(strip, strip_coef)
    rest = jnp.zeros_like(spread[:, STEPS:])
    edge = jnp.where(
        odd,
        jnp.concatenate([rest, edge[:, :STEPS]], 1),
        jnp.concatenate([edge[:, STEPS:], rest], 1),
    )
    return controls + (spread + edge)


def solution(mesh):
    placed = (
        P("mem", "tile", None),
        P("mem", None, "tile", None),
        P(None, "tile", None),
        P("tile", None),
        P("tile", None),
        P("tile", None),
        P("tile", None),
    )
    return jax.shard_map(
        per_device, mesh=mesh, in_specs=placed, out_specs=P("mem", "tile", None), check_vma=False
    )
```

```python
import jax
import jax.numpy as jnp
from jax import lax
from jax.sharding import PartitionSpec as P

STEPS = 4


def exchange(part, width):
    count = lax.axis_size("tile")
    head = part[..., :width, :]
    tail = part[..., -width:, :]
    if count % 2:
        above = lax.ppermute(tail, "tile", [(i, i + 1) for i in range(count - 1)])
        below = lax.ppermute(head, "tile", [(i + 1, i) for i in range(count - 1)])
        return jnp.concatenate([above, part, below], -2)
    odd = lax.axis_index("tile") % 2 == 1
    pairs = lambda first: [(i, i + 1) for i in range(first, count - 1, 2)] + [
        (i + 1, i) for i in range(first, count - 1, 2)
    ]
    far = lax.ppermute(jnp.where(odd, tail, head), "tile", pairs(1))
    near = lax.ppermute(jnp.where(odd, head, tail), "tile", pairs(0))
    above = jnp.where(odd, near, far)
    below = jnp.where(odd, far, near)
    return jnp.concatenate([above, part, below], -2)


def split_exchange(part, width):
    count = lax.axis_size("tile")
    head = part[..., :width, :]
    tail = part[..., -width:, :]
    odd = lax.axis_index("tile") % 2 == 1
    pairs = lambda first: [(i, i + 1) for i in range(first, count - 1, 2)] + [
        (i + 1, i) for i in range(first, count - 1, 2)
    ]
    far = lax.ppermute(jnp.where(odd, tail, head), "tile", pairs(1))
    near = lax.ppermute(jnp.where(odd, head, tail), "tile", pairs(0))
    return near, far, odd


def near_band(part, near, odd):
    zero = jnp.zeros_like(near)
    return jnp.concatenate([jnp.where(odd, near, zero), part, jnp.where(odd, zero, near)], -2)


def full_band(part, near, far, odd):
    return jnp.concatenate([jnp.where(odd, near, far), part, jnp.where(odd, far, near)], -2)


def mem_sum(part):
    count = lax.axis_size("mem")
    if count & (count - 1):
        return lax.psum(part, "mem")

    def partner(stride):
        return lax.ppermute(part, "mem", [(i, i ^ stride) for i in range(count)])

    stride = 1
    while stride < count:
        if stride * 2 < count:
            near, far, both = partner(stride), partner(2 * stride), partner(3 * stride)
            part = (part + near) + (far + both)
            stride *= 4
        else:
            part = part + partner(stride)
            stride *= 2
    return part


def diffuse(values, row_coef, col_coef):
    row_flux = row_coef[..., :-1, :] * (values[..., 1:, :] - values[..., :-1, :])
    col_flux = col_coef[..., :, :-1] * (values[..., :, 1:] - values[..., :, :-1])
    zeros_row = jnp.zeros_like(values[..., :1, :])
    zeros_col = jnp.zeros_like(values[..., :, :1])
    values = (
        values
        + jnp.concatenate([row_flux, zeros_row], -2)
        - jnp.concatenate([zeros_row, row_flux], -2)
    )
    return (
        values
        + jnp.concatenate([col_flux, zeros_col], -1)
        - jnp.concatenate([zeros_col, col_flux], -1)
    )


def localize(field, coef_band):
    for repeat in range(STEPS):
        field = diffuse(field, coef_band[0], coef_band[1])
    return field


def localize_inner(field, coef_band):
    for repeat in range(STEPS):
        field = diffuse(field, coef_band[0], coef_band[1])[..., 1:-1, :]
        coef_band = coef_band[..., 1:-1, :]
    return field


def per_device(controls, perturbations, jacobian, obs_weight, radar_mask, row_faces, col_faces):
    members, row_count = controls.shape[:2]
    row_index = lax.axis_index("tile") * row_count + lax.broadcasted_iota(
        jnp.int32, row_faces.shape, 0
    )
    row_coef = jnp.where(
        row_index < row_count * lax.axis_size("tile") - 1, row_faces, jnp.zeros_like(row_faces)
    )
    mix = jnp.sum(perturbations.astype(jnp.float32) * jacobian[None], axis=1)
    stacked = jnp.concatenate([controls, row_coef[None], col_faces[None]], 0)
    if lax.axis_size("tile") % 2:
        band = exchange(stacked, STEPS)
        field, coef_band = band[:members], band[members:]
        localized = localize(field, coef_band)[:, STEPS : STEPS + row_count]
        reflect = mem_sum(jnp.sum(mix * localized, 0))
        weighted = radar_mask.astype(jnp.float32) * obs_weight * reflect
        sensitivity = exchange(mix * weighted[None], STEPS)
        return controls + localize(sensitivity, coef_band)[:, STEPS : STEPS + row_count]
    near, far, odd = split_exchange(stacked, STEPS)
    partial = near_band(stacked, near, odd)
    main = localize(partial[:members], partial[members:])[:, STEPS : STEPS + row_count]
    inner = jnp.sum(mix * main, 0)
    inner, far = lax.optimization_barrier((inner, far))
    band = full_band(stacked, near, far, odd)
    coef_band = band[members:]
    strip = jnp.where(odd, band[:, row_count - STEPS :], band[:, : 3 * STEPS])
    edge = localize_inner(strip[:members], strip[members:])
    edge_mix = jnp.where(odd, mix[:, row_count - STEPS :], mix[:, :STEPS])
    outer = jnp.sum(edge_mix * edge, 0)
    partial_sum = jnp.where(
        odd,
        jnp.concatenate([inner[: row_count - STEPS], outer], 0),
        jnp.concatenate([outer, inner[STEPS:]], 0),
    )
    reflect = mem_sum(partial_sum)
    weighted = radar_mask.astype(jnp.float32) * obs_weight * reflect
    near, far, odd = split_exchange(mix * weighted[None], STEPS)
    spread = localize(near_band(mix * weighted[None], near, odd), coef_band)
    spread = spread[:, STEPS : STEPS + row_count]
    spread, far = lax.optimization_barrier((spread, far))
    zero = jnp.zeros_like(far)
    strip = jnp.where(odd, jnp.concatenate([zero, far], 1), jnp.concatenate([far, zero], 1))
    strip_coef = jnp.where(odd, coef_band[:, row_count:], coef_band[:, : 2 * STEPS])
    edge = localize(strip, strip_coef)
    rest = jnp.zeros_like(spread[:, STEPS:])
    edge = jnp.where(
        odd,
        jnp.concatenate([rest, edge[:, :STEPS]], 1),
        jnp.concatenate([edge[:, STEPS:], rest], 1),
    )
    return controls + (spread + edge)


def solution(mesh):
    placed = (
        P("mem", "tile", None),
        P("mem", None, "tile", None),
        P(None, "tile", None),
        P("tile", None),
        P("tile", None),
        P("tile", None),
        P("tile", None),
    )
    return jax.shard_map(
        per_device, mesh=mesh, in_specs=placed, out_specs=P("mem", "tile", None), check_vma=False
    )
```

```python
import jax
import jax.numpy as jnp
from jax import lax
from jax.sharding import PartitionSpec as P

STEPS = 4


def exchange(part, width):
    count = lax.axis_size("tile")
    head = part[..., :width, :]
    tail = part[..., -width:, :]
    if count % 2:
        above = lax.ppermute(tail, "tile", [(i, i + 1) for i in range(count - 1)])
        below = lax.ppermute(head, "tile", [(i + 1, i) for i in range(count - 1)])
        return jnp.concatenate([above, part, below], -2)
    odd = lax.axis_index("tile") % 2 == 1
    pairs = lambda first: [(i, i + 1) for i in range(first, count - 1, 2)] + [
        (i + 1, i) for i in range(first, count - 1, 2)
    ]
    far = lax.ppermute(jnp.where(odd, tail, head), "tile", pairs(1))
    near = lax.ppermute(jnp.where(odd, head, tail), "tile", pairs(0))
    above = jnp.where(odd, near, far)
    below = jnp.where(odd, far, near)
    return jnp.concatenate([above, part, below], -2)


def split_exchange(part, width):
    count = lax.axis_size("tile")
    head = part[..., :width, :]
    tail = part[..., -width:, :]
    odd = lax.axis_index("tile") % 2 == 1
    pairs = lambda first: [(i, i + 1) for i in range(first, count - 1, 2)] + [
        (i + 1, i) for i in range(first, count - 1, 2)
    ]
    far = lax.ppermute(jnp.where(odd, tail, head), "tile", pairs(1))
    near = lax.ppermute(jnp.where(odd, head, tail), "tile", pairs(0))
    return near, far, odd


def near_band(part, near, odd):
    zero = jnp.zeros_like(near)
    return jnp.concatenate([jnp.where(odd, near, zero), part, jnp.where(odd, zero, near)], -2)


def full_band(part, near, far, odd):
    return jnp.concatenate([jnp.where(odd, near, far), part, jnp.where(odd, far, near)], -2)


def mem_sum(part):
    count = lax.axis_size("mem")
    if count & (count - 1):
        return lax.psum(part, "mem")

    def partner(stride):
        return lax.ppermute(part, "mem", [(i, i ^ stride) for i in range(count)])

    stride = 1
    while stride < count:
        if stride * 2 < count:
            near, far, both = partner(stride), partner(2 * stride), partner(3 * stride)
            part = (part + near) + (far + both)
            stride *= 4
        else:
            part = part + partner(stride)
            stride *= 2
    return part


def diffuse(values, row_coef, col_coef):
    row_flux = row_coef[..., :-1, :] * (values[..., 1:, :] - values[..., :-1, :])
    col_flux = col_coef[..., :, :-1] * (values[..., :, 1:] - values[..., :, :-1])
    zeros_row = jnp.zeros_like(values[..., :1, :])
    zeros_col = jnp.zeros_like(values[..., :, :1])
    values = (
        values
        + jnp.concatenate([row_flux, zeros_row], -2)
        - jnp.concatenate([zeros_row, row_flux], -2)
    )
    return (
        values
        + jnp.concatenate([col_flux, zeros_col], -1)
        - jnp.concatenate([zeros_col, col_flux], -1)
    )


def localize(field, coef_band):
    for repeat in range(STEPS):
        field = diffuse(field, coef_band[0], coef_band[1])
    return field


def localize_inner(field, coef_band):
    for repeat in range(STEPS):
        field = diffuse(field, coef_band[0], coef_band[1])[..., 1:-1, :]
        coef_band = coef_band[..., 1:-1, :]
    return field


def per_device(controls, perturbations, jacobian, obs_weight, radar_mask, row_faces, col_faces):
    members, row_count = controls.shape[:2]
    row_index = lax.axis_index("tile") * row_count + lax.broadcasted_iota(
        jnp.int32, row_faces.shape, 0
    )
    row_coef = jnp.where(
        row_index < row_count * lax.axis_size("tile") - 1, row_faces, jnp.zeros_like(row_faces)
    )
    mix = jnp.sum(perturbations.astype(jnp.float32) * jacobian[None], axis=1)
    stacked = jnp.concatenate([controls, row_coef[None], col_faces[None]], 0)
    if lax.axis_size("tile") % 2:
        band = exchange(stacked, STEPS)
        field, coef_band = band[:members], band[members:]
        localized = localize(field, coef_band)[:, STEPS : STEPS + row_count]
        reflect = mem_sum(jnp.sum(mix * localized, 0))
        weighted = radar_mask.astype(jnp.float32) * obs_weight * reflect
        sensitivity = exchange(mix * weighted[None], STEPS)
        return controls + localize(sensitivity, coef_band)[:, STEPS : STEPS + row_count]
    near, far, odd = split_exchange(stacked, STEPS)
    partial = near_band(stacked, near, odd)
    main = localize(partial[:members], partial[members:])[:, STEPS : STEPS + row_count]
    inner = jnp.sum(mix * main, 0)
    inner, far = lax.optimization_barrier((inner, far))
    coef_band = full_band(stacked[members:], near[members:], far[members:], odd)
    strip = jnp.where(
        odd,
        jnp.concatenate([stacked[:, row_count - 2 * STEPS :], far], 1),
        jnp.concatenate([far, stacked[:, : 2 * STEPS]], 1),
    )
    edge = localize_inner(strip[:members], strip[members:])
    edge_mix = jnp.where(odd, mix[:, row_count - STEPS :], mix[:, :STEPS])
    outer = jnp.sum(edge_mix * edge, 0)
    partial_sum = jnp.where(
        odd,
        jnp.concatenate([inner[: row_count - STEPS], outer], 0),
        jnp.concatenate([outer, inner[STEPS:]], 0),
    )
    reflect = mem_sum(partial_sum)
    weighted = radar_mask.astype(jnp.float32) * obs_weight * reflect
    near, far, odd = split_exchange(mix * weighted[None], STEPS)
    spread = localize(near_band(mix * weighted[None], near, odd), coef_band)
    spread = spread[:, STEPS : STEPS + row_count]
    spread, far = lax.optimization_barrier((spread, far))
    zero = jnp.zeros_like(far)
    strip = jnp.where(odd, jnp.concatenate([zero, far], 1), jnp.concatenate([far, zero], 1))
    strip_coef = jnp.where(odd, coef_band[:, row_count:], coef_band[:, : 2 * STEPS])
    edge = localize(strip, strip_coef)
    rest = jnp.zeros_like(spread[:, STEPS:])
    edge = jnp.where(
        odd,
        jnp.concatenate([rest, edge[:, :STEPS]], 1),
        jnp.concatenate([edge[:, STEPS:], rest], 1),
    )
    return controls + (spread + edge)


def solution(mesh):
    placed = (
        P("mem", "tile", None),
        P("mem", None, "tile", None),
        P(None, "tile", None),
        P("tile", None),
        P("tile", None),
        P("tile", None),
        P("tile", None),
    )
    return jax.shard_map(
        per_device, mesh=mesh, in_specs=placed, out_specs=P("mem", "tile", None), check_vma=False
    )
```

```python
import jax
import jax.numpy as jnp
from jax import lax
from jax.sharding import PartitionSpec as P

STEPS = 4


def exchange(part, width):
    count = lax.axis_size("tile")
    head = part[..., :width, :]
    tail = part[..., -width:, :]
    if count % 2:
        above = lax.ppermute(tail, "tile", [(i, i + 1) for i in range(count - 1)])
        below = lax.ppermute(head, "tile", [(i + 1, i) for i in range(count - 1)])
        return jnp.concatenate([above, part, below], -2)
    odd = lax.axis_index("tile") % 2 == 1
    pairs = lambda first: [(i, i + 1) for i in range(first, count - 1, 2)] + [
        (i + 1, i) for i in range(first, count - 1, 2)
    ]
    far = lax.ppermute(jnp.where(odd, tail, head), "tile", pairs(1))
    near = lax.ppermute(jnp.where(odd, head, tail), "tile", pairs(0))
    above = jnp.where(odd, near, far)
    below = jnp.where(odd, far, near)
    return jnp.concatenate([above, part, below], -2)


def split_exchange(part, width):
    count = lax.axis_size("tile")
    head = part[..., :width, :]
    tail = part[..., -width:, :]
    odd = lax.axis_index("tile") % 2 == 1
    pairs = lambda first: [(i, i + 1) for i in range(first, count - 1, 2)] + [
        (i + 1, i) for i in range(first, count - 1, 2)
    ]
    far = lax.ppermute(jnp.where(odd, tail, head), "tile", pairs(1))
    near = lax.ppermute(jnp.where(odd, head, tail), "tile", pairs(0))
    return near, far, odd


def near_band(part, near, odd):
    zero = jnp.zeros_like(near)
    return jnp.concatenate([jnp.where(odd, near, zero), part, jnp.where(odd, zero, near)], -2)


def full_band(part, near, far, odd):
    return jnp.concatenate([jnp.where(odd, near, far), part, jnp.where(odd, far, near)], -2)


def mem_sum(part):
    count = lax.axis_size("mem")
    if count & (count - 1):
        return lax.psum(part, "mem")

    def partner(stride):
        return lax.ppermute(part, "mem", [(i, i ^ stride) for i in range(count)])

    stride = 1
    while stride < count:
        if stride * 2 < count:
            near, far, both = partner(stride), partner(2 * stride), partner(3 * stride)
            part = (part + near) + (far + both)
            stride *= 4
        else:
            part = part + partner(stride)
            stride *= 2
    return part


def diffuse(values, row_coef, col_coef):
    row_flux = row_coef[..., :-1, :] * (values[..., 1:, :] - values[..., :-1, :])
    col_flux = col_coef[..., :, :-1] * (values[..., :, 1:] - values[..., :, :-1])
    zeros_row = jnp.zeros_like(values[..., :1, :])
    zeros_col = jnp.zeros_like(values[..., :, :1])
    values = (
        values
        + jnp.concatenate([row_flux, zeros_row], -2)
        - jnp.concatenate([zeros_row, row_flux], -2)
    )
    return (
        values
        + jnp.concatenate([col_flux, zeros_col], -1)
        - jnp.concatenate([zeros_col, col_flux], -1)
    )


def localize(field, coef_band):
    for repeat in range(STEPS):
        field = diffuse(field, coef_band[0], coef_band[1])
    return field


def localize_inner(field, coef_band):
    for repeat in range(STEPS):
        field = diffuse(field, coef_band[0], coef_band[1])[..., 1:-1, :]
        coef_band = coef_band[..., 1:-1, :]
    return field


def per_device(controls, perturbations, jacobian, obs_weight, radar_mask, row_faces, col_faces):
    members, row_count = controls.shape[:2]
    row_index = lax.axis_index("tile") * row_count + lax.broadcasted_iota(
        jnp.int32, row_faces.shape, 0
    )
    row_coef = jnp.where(
        row_index < row_count * lax.axis_size("tile") - 1, row_faces, jnp.zeros_like(row_faces)
    )
    mix = jnp.sum(perturbations.astype(jnp.float32) * jacobian[None], axis=1)
    stacked = jnp.concatenate([controls, row_coef[None], col_faces[None]], 0)
    if lax.axis_size("tile") % 2:
        band = exchange(stacked, STEPS)
        field, coef_band = band[:members], band[members:]
        localized = localize(field, coef_band)[:, STEPS : STEPS + row_count]
        reflect = mem_sum(jnp.sum(mix * localized, 0))
        weighted = radar_mask.astype(jnp.float32) * obs_weight * reflect
        sensitivity = exchange(mix * weighted[None], STEPS)
        return controls + localize(sensitivity, coef_band)[:, STEPS : STEPS + row_count]
    near, far, odd = split_exchange(stacked, STEPS)
    partial = near_band(stacked, near, odd)
    main = localize(partial[:members], partial[members:])[:, STEPS : STEPS + row_count]
    inner = jnp.sum(mix * main, 0)
    inner, far = lax.optimization_barrier((inner, far))
    coef_band = full_band(stacked[members:], near[members:], far[members:], odd)
    strip = jnp.where(
        odd,
        jnp.concatenate([stacked[:, row_count - 2 * STEPS :], far], 1),
        jnp.concatenate([far, stacked[:, : 2 * STEPS]], 1),
    )
    edge = localize_inner(strip[:members], strip[members:])
    edge_mix = jnp.where(odd, mix[:, row_count - STEPS :], mix[:, :STEPS])
    outer = jnp.sum(edge_mix * edge, 0)
    partial_sum = jnp.where(
        odd,
        jnp.concatenate([inner[: row_count - STEPS], outer], 0),
        jnp.concatenate([outer, inner[STEPS:]], 0),
    )
    reflect = mem_sum(partial_sum)
    weighted = radar_mask.astype(jnp.float32) * obs_weight * reflect
    coef_far = far[members:]
    near, far, odd = split_exchange(mix * weighted[None], STEPS)
    spread = localize(near_band(mix * weighted[None], near, odd), coef_band)
    spread = spread[:, STEPS : STEPS + row_count]
    spread, far = lax.optimization_barrier((spread, far))
    zero = jnp.zeros_like(far)
    strip = jnp.where(odd, jnp.concatenate([zero, far], 1), jnp.concatenate([far, zero], 1))
    strip_coef = jnp.where(
        odd,
        jnp.concatenate([stacked[members:, row_count - STEPS :], coef_far], 1),
        jnp.concatenate([coef_far, stacked[members:, :STEPS]], 1),
    )
    edge = localize(strip, strip_coef)
    rest = jnp.zeros_like(spread[:, STEPS:])
    edge = jnp.where(
        odd,
        jnp.concatenate([rest, edge[:, :STEPS]], 1),
        jnp.concatenate([edge[:, STEPS:], rest], 1),
    )
    return controls + (spread + edge)


def solution(mesh):
    placed = (
        P("mem", "tile", None),
        P("mem", None, "tile", None),
        P(None, "tile", None),
        P("tile", None),
        P("tile", None),
        P("tile", None),
        P("tile", None),
    )
    return jax.shard_map(
        per_device, mesh=mesh, in_specs=placed, out_specs=P("mem", "tile", None), check_vma=False
    )
```
